256 devices in a mesh: seq: 16 (over x, y), tensor: 16 (over z, core).
Axes of the slice: x: 4, y: 4, z: 8, core: 2. Of those that a mesh axis runs over, the one named last changes fastest.
Arguments:
- queries: bfloat16 [16384, 4096], P(('seq', 'tensor')), may hold values from -6 to 6
- key_rows: bfloat16 [16384, 4096], P(('seq', 'tensor')), may hold values from -6 to 6
- values: bfloat16 [16384, 4096], P(('seq', 'tensor')), may hold values from -6 to 6
- input_gate: bfloat16 [16384, 4], P(('seq', 'tensor')), may hold values from -3 to 1
- forget_gate: bfloat16 [16384, 4], P(('seq', 'tensor')), may hold values from 0 to 16
- segment_ids: int32 [16384], P('seq'), may hold values from 0 to 3, never falling along the last dimension, each value on 1 to 8192 neighbouring positions
- output_gate: bfloat16 [16384, 4096], P(('seq', 'tensor')), may hold values from -6 to 6
- norm_gain: float32 [4096], replicated, may hold values from 0.5 to 1.5
Outputs:
- gated_out: bfloat16 [16384, 4096], P(('seq', 'tensor'))
The draws below stay inside these ranges and needn't reach their ends.
Inputs may be any that keep to these rules, and one draw needn't show every extreme that they name: `segment_ids`: non-decreasing along the tokens; each of the 4 prompts holds 1 to 8192 consecutive tokens, one exactly 8192.
All inputs are finite; a program needn't handle non-finite values.
Results may differ from the reference program's by a relative error of at most 0.005.
Values may be sent and summed in bfloat16 or wider, within the bound.
No kernel may reach another device: no remote copies, remote signals or barrier semaphores. Data moves between devices by JAX's collectives and lax.ppermute only.
A program may use at most 64 MiB of HBM per device.

```python
import math
import jax
import jax.numpy as jnp
import numpy as np
from jax import lax

HEADS = 4
HEAD_DIM = 1024
INNER = 4096
TOK_DEV = 1024
BLOCK = 256
PROMPTS = 4
PACKED_TOKENS = 16384
MAX_LEN = 8192


def draw_forget_gate(key, part):
    key_order = jax.random.fold_in(key, 101)
    key_rough = jax.random.fold_in(key, 202)
    key_block = jax.random.fold_in(key, 303)
    key_spike = jax.random.fold_in(key, 404)
    order = jax.random.permutation(key_order, HEADS)
    slow_count = HEADS // 2
    sluggish_part = (order < slow_count).astype(jnp.float32)
    rough = jnp.exp(jax.random.uniform(key_rough, (PACKED_TOKENS, HEADS), jnp.float32, -0.7, 0.7))
    block_count = PACKED_TOKENS // TOK_DEV
    block_factor = jnp.exp(jax.random.uniform(key_block, (block_count, 1, HEADS), jnp.float32, -0.7, 0.7))
    block_factor = jnp.broadcast_to(block_factor, (block_count, TOK_DEV, HEADS)).reshape(PACKED_TOKENS, HEADS)
    base_rate = sluggish_part * (1.6 / PACKED_TOKENS) + (1.0 - sluggish_part) * (1.0 / 40.0)
    decay_rate = base_rate[None, :] * rough * block_factor
    token_positions = jax.random.randint(key_spike, (6,), 0, PACKED_TOKENS)
    spike_amount = jnp.any(jnp.arange(PACKED_TOKENS)[:, None] == token_positions[None, :], axis=1)
    decay_rate = jnp.where(spike_amount[:, None], sluggish_part[None, :] * 0.33 + (1.0 - sluggish_part[None, :]) * decay_rate, decay_rate)
    return jnp.log((1.0 - decay_rate) / decay_rate).astype(jnp.bfloat16)


def block_levels(rng, extent, pieces, low, high):
    factor_of = 1.0
    for dim, shards_of in pieces:
        heights = jax.random.uniform(jax.random.fold_in(jax.random.fold_in(rng, 6), dim), (shards_of,), jnp.float32, low / len(pieces), high / len(pieces))
        factor_of = factor_of * jnp.repeat(jnp.exp(heights), extent[dim] // shards_of).reshape((-1,) + (1,) * (len(extent) - 1 - dim))
    return factor_of


def split_up(amount, total, reach, skew):
    weights = [(1 << 20) // math.isqrt(standing ** skew) + 1 for standing in range(2, amount + 1)]
    surplus, given = total - reach - (amount - 1), [1] * (amount - 1)
    while surplus > 0:
        free = [i for i in range(amount - 1) if given[i] < reach]
        mass, remaining = sum([weights[i] for i in free]), surplus
        for i in free:
            more = min(reach - given[i], max(1, remaining * weights[i] // mass), surplus)
            given[i] = given[i] + more
            surplus = surplus - more
    return np.array([reach] + given)


def uneven_parts(stream_key, amount, total, limit, slope):
    if amount == 2:
        one = jax.random.randint(stream_key, (), max(1, total - limit), min(limit, total - 1) + 1)
        return jnp.stack([one, total - one])
    tallies = jnp.asarray(split_up(amount, total, limit, slope), jnp.int32)
    couples = (amount - 1) // 2
    giver, sink = tallies[1:1 + 2 * couples:2], tallies[2:2 + 2 * couples:2]
    room = jnp.minimum(giver - 1, limit - sink)
    shifted = jax.random.randint(jax.random.fold_in(stream_key, 1), (couples,), 0, 1 << 20) % (room + 1)
    tallies = tallies.at[1:1 + 2 * couples:2].set(giver - shifted).at[2:2 + 2 * couples:2].set(sink + shifted)
    return tallies[jax.random.permutation(jax.random.fold_in(stream_key, 2), amount)]


def normal_values(stream_key, shape, spread, bound, shards=(), kind=jnp.bfloat16):
    gain = block_levels(stream_key, shape, shards, -0.22, 0.18) if shards else 1.0
    drawn = jax.random.normal(stream_key, shape, jnp.float32) * spread * gain
    return jnp.minimum(jnp.maximum(drawn, -bound), bound).astype(kind)


def setup_inputs(seed: int = 0) -> dict:
    seeds = jax.random.split(jax.random.key(seed), 9)
    return {
        "queries": normal_values(seeds[0], (PACKED_TOKENS, INNER), 1.0, 6.0, ((0, 256),)),
        "key_rows": normal_values(seeds[1], (PACKED_TOKENS, INNER), 1.0, 6.0, ((0, 256),)),
        "values": normal_values(seeds[2], (PACKED_TOKENS, INNER), 1.0, 6.0, ((0, 256),)),
        "input_gate": jnp.clip(-3.0 + 4.0 * jax.random.uniform(seeds[3], (PACKED_TOKENS, HEADS), jnp.float32) ** block_levels(seeds[3], (PACKED_TOKENS, HEADS), ((0, 256),), -0.2, 0.2), -3.0, 1.0).astype(jnp.bfloat16),
        "forget_gate": draw_forget_gate(jax.random.fold_in(seeds[8], 71), 0),
        "segment_ids": jnp.searchsorted(jnp.cumsum(uneven_parts(seeds[5], PROMPTS, PACKED_TOKENS, MAX_LEN, 2)), jnp.arange(PACKED_TOKENS), side="right").astype(jnp.int32),
        "output_gate": normal_values(seeds[6], (PACKED_TOKENS, INNER), 1.0, 6.0, ((0, 256),)),
        "norm_gain": jnp.clip(1.0 + 0.1 * jax.random.normal(seeds[7], (INNER,), jnp.float32), 0.5, 1.5),
    }


precise = lax.Precision.HIGHEST

def reference(queries, key_rows, values, input_gate, forget_gate, segment_ids, output_gate, norm_gain):
    key_scale = 1.0 / math.sqrt(HEAD_DIM)
    blocks_all = PACKED_TOKENS // BLOCK
    query_float = queries.astype(jnp.float32).reshape(blocks_all, BLOCK, HEADS, HEAD_DIM)
    keys_f = key_rows.astype(jnp.float32).reshape(blocks_all, BLOCK, HEADS, HEAD_DIM) * key_scale
    values_f = values.astype(jnp.float32).reshape(blocks_all, BLOCK, HEADS, HEAD_DIM)
    gate_in = input_gate.astype(jnp.float32).reshape(blocks_all, BLOCK, HEADS)
    log_forget = jax.nn.log_sigmoid(forget_gate.astype(jnp.float32)).reshape(blocks_all, BLOCK, HEADS)
    segments = segment_ids.reshape(blocks_all, BLOCK)
    row_ids = jnp.arange(BLOCK, dtype=jnp.int32)
    causal = row_ids[:, None] >= row_ids[None, :]

    def span_step(carry, block_in):
        cell_state, norm_vec, prev_seg = carry
        query_b, key_b, value_b, gate_b, forget_b, seg_b = block_in
        cumulative = jnp.cumsum(forget_b, axis=0)
        allowed = (causal & (seg_b[:, None] == seg_b[None, :]))[None]
        cum_heads = cumulative.T
        exponent = cum_heads[:, :, None] - cum_heads[:, None, :] + gate_b.T[:, None, :]
        weights = jnp.where(allowed, jnp.exp(jnp.where(allowed, exponent, 0.0)), 0.0)
        scores = jnp.einsum('ihd,jhd->hij', query_b, key_b, precision=precise)
        weighted = weights * scores
        numerator = jnp.einsum('hij,jhd->ihd', weighted, value_b, precision=precise)
        q_norm = lax.optimization_barrier(jnp.sum(weighted, axis=2)).T
        carried = jnp.exp(cumulative) * (seg_b == prev_seg).astype(jnp.float32)[:, None]
        numerator = numerator + carried[:, :, None] * jnp.einsum('ihk,hkd->ihd', query_b, cell_state, precision=precise)
        q_norm = q_norm + carried * jnp.einsum('ihk,hk->ih', query_b, norm_vec, precision=precise)
        last_seg = seg_b[BLOCK - 1]
        tail_weight = jnp.exp(cumulative[BLOCK - 1][None, :] - cumulative + gate_b) * (seg_b == last_seg).astype(jnp.float32)[:, None]
        keep_factor = jnp.exp(cumulative[BLOCK - 1]) * (last_seg == prev_seg).astype(jnp.float32)
        scaled_keys = key_b * tail_weight[:, :, None]
        cell_state = keep_factor[:, None, None] * cell_state + jnp.einsum('jhk,jhd->hkd', scaled_keys, value_b, precision=precise)
        norm_vec = keep_factor[:, None] * norm_vec + lax.optimization_barrier(jnp.sum(scaled_keys, axis=0))
        hidden = (numerator / jnp.maximum(jnp.abs(q_norm), 1.0)[:, :, None]).astype(jnp.bfloat16)
        return ((cell_state, norm_vec, last_seg), hidden)
    initial = (jnp.zeros((HEADS, HEAD_DIM, HEAD_DIM), jnp.float32), jnp.zeros((HEADS, HEAD_DIM), jnp.float32), jnp.array(-1, jnp.int32))
    unused, hidden = lax.scan(span_step, initial, (query_float, keys_f, values_f, gate_in, log_forget, segments))
    hidden_f = hidden.astype(jnp.float32).reshape(PACKED_TOKENS, HEADS, HEAD_DIM)
    mean_val = lax.optimization_barrier(jnp.mean(hidden_f, axis=2, keepdims=True))
    centered = hidden_f - mean_val
    variance = lax.optimization_barrier(jnp.mean(centered * centered, axis=2, keepdims=True))
    normed = (centered * lax.rsqrt(variance + 1e-05)).reshape(PACKED_TOKENS, INNER)
    return (normed * norm_gain * jax.nn.silu(output_gate.astype(jnp.float32))).astype(jnp.bfloat16)
```

```python
import math

import jax
import jax.numpy as jnp
from jax import lax
from jax.sharding import PartitionSpec as P

BLOCK = 256


precise = lax.Precision.HIGHEST


def shifted(value, axis, steps):
    count = lax.axis_size(axis)
    initial, last = (max(0, -steps), min(count, count - steps))
    return lax.ppermute(value, axis, [(source, source + steps) for source in range(initial, last)])


def meta_row(head_dim, column_count):
    return head_dim + head_dim // column_count


def pack_summary(query_all, key_all, value_all, gate_in, log_forget, segment_ids, key_scale):
    head_dim = key_all.shape[1]
    column_count = value_all.shape[1]
    cumulative = jnp.cumsum(log_forget)
    total_log = cumulative[-1]
    first_seg = segment_ids[0]
    last_seg = segment_ids[-1]
    tail_weight = jnp.exp(total_log - cumulative + gate_in) * (segment_ids == last_seg).astype(
        jnp.float32
    )
    scaled_keys = key_all.astype(jnp.float32) * (key_scale * tail_weight)[:, None]
    state = jnp.dot(scaled_keys.T, value_all.astype(jnp.float32), precision=precise)
    norm = jnp.sum(scaled_keys, axis=0)
    decay = jnp.exp(total_log) * (last_seg == first_seg).astype(jnp.float32)
    norm_rows = head_dim // column_count
    rows = meta_row(head_dim, column_count) + 1
    padded = -(-rows // 8) * 8
    lane = jnp.arange(column_count)
    meta = jnp.where(
        lane == 0,
        decay,
        jnp.where(
            lane == 1,
            (first_seg + 1).astype(jnp.float32),
            jnp.where(lane == 2, (last_seg + 1).astype(jnp.float32), 0.0),
        ),
    )
    filler = jnp.zeros((padded - rows, column_count), jnp.float32)
    return jnp.concatenate(
        [state, norm.reshape(norm_rows, column_count), meta[None, :], filler], axis=0
    )


def combine_packed(earlier, later, head_dim):
    column_count = earlier.shape[1]
    row = meta_row(head_dim, column_count)
    e_decay, e_first, e_last = earlier[row, 0], earlier[row, 1], earlier[row, 2]
    l_decay, l_first, l_last = later[row, 0], later[row, 1], later[row, 2]
    linked = jnp.where((e_last == l_first) | (e_last <= 0.0) | (l_first <= 0.0), 1.0, 0.0)
    factor = jnp.where(l_first <= 0.0, 1.0, l_decay * linked)
    decay_part = jnp.where(e_first <= 0.0, l_decay, e_decay * factor)
    first_seg = jnp.where(e_first <= 0.0, l_first, e_first)
    last_seg = jnp.where(l_last <= 0.0, e_last, l_last)
    body = factor * earlier + later
    lane = jnp.arange(column_count)[None, :]
    rows = jnp.arange(earlier.shape[0])[:, None]
    meta = jnp.where(lane == 0, decay_part, jnp.where(lane == 1, first_seg, last_seg))
    return jnp.where((rows == row) & (lane < 3), meta, body)


def on_device(
    queries, key_rows, values, input_gate, forget_gate, segment_ids, output_gate, norm_gain
):
    tensor_size = lax.axis_size("tensor")
    row_count, inner = queries.shape
    head_count = input_gate.shape[1]
    head_dim = inner // head_count
    group_size = tensor_size // head_count
    column_count = head_dim // group_size

    def spread_heads(array, width):
        shaped = array.reshape(row_count, head_count, 1, width)
        return jnp.broadcast_to(shaped, (row_count, head_count, group_size, width)).reshape(
            row_count, tensor_size, width
        )

    query_send = spread_heads(queries, head_dim)
    key_send = spread_heads(key_rows, head_dim)
    value_send = values.reshape(row_count, tensor_size, column_count)
    gate_send = spread_heads(jnp.stack([input_gate, forget_gate], axis=2), 2)
    query_all, key_all, value_all, gate_all = (
        lax.all_to_all(query_send, "tensor", split_axis=1, concat_axis=0, tiled=True),
        lax.all_to_all(key_send, "tensor", split_axis=1, concat_axis=0, tiled=True),
        lax.all_to_all(value_send, "tensor", split_axis=1, concat_axis=0, tiled=True),
        lax.all_to_all(gate_send, "tensor", split_axis=1, concat_axis=0, tiled=True),
    )
    token_count = query_all.shape[0]
    query_all = query_all.reshape(token_count, head_dim)
    key_all = key_all.reshape(token_count, head_dim)
    value_all = value_all.reshape(token_count, column_count)
    gate_f = gate_all.reshape(token_count, 2).astype(jnp.float32)
    gate_in = gate_f[:, 0]
    log_forget = jax.nn.log_sigmoid(gate_f[:, 1])
    block_count = token_count // BLOCK
    key_scale = 1.0 / math.sqrt(head_dim)
    first_seg = segment_ids[0]

    packed = pack_summary(
        query_all, key_all, value_all, gate_in, log_forget, segment_ids, key_scale
    )
    scanned = packed
    shift = 1
    while shift < lax.axis_size("seq"):
        scanned = combine_packed(shifted(scanned, "seq", shift), scanned, head_dim)
        shift *= 2
    incoming = shifted(scanned, "seq", 1)
    in_row = meta_row(head_dim, column_count)
    in_state = incoming[:head_dim]
    in_norm = incoming[head_dim:in_row].reshape(head_dim)
    in_last = incoming[in_row, 2]

    row_ids = jnp.arange(BLOCK, dtype=jnp.int32)
    causal = row_ids[:, None] >= row_ids[None, :]

    def span_step(carry, block_in):
        cell_state, norm_vec, prev_seg, total_log = carry
        query_b, key_b, value_b, gate_b, forget_b, seg_b = block_in
        cumulative = jnp.cumsum(forget_b)
        allowed = causal & (seg_b[:, None] == seg_b[None, :])
        exponent = cumulative[:, None] - cumulative[None, :] + gate_b[None, :]
        weights = jnp.where(allowed, jnp.exp(jnp.where(allowed, exponent, 0.0)), 0.0)
        scores = (
            jnp.einsum("id,jd->ij", query_b, key_b, preferred_element_type=jnp.float32) * key_scale
        )
        weighted = weights * scores
        query_float = query_b.astype(jnp.float32)
        key_f = key_b.astype(jnp.float32) * key_scale
        value_f = value_b.astype(jnp.float32)
        numerator = jnp.dot(weighted, value_f, precision=precise)
        carried = jnp.exp(cumulative) * (seg_b == prev_seg).astype(jnp.float32)
        numerator = numerator + carried[:, None] * jnp.dot(
            query_float, cell_state, precision=precise
        )
        q_norm = jnp.sum(weighted, axis=1) + carried * jnp.dot(
            query_float, norm_vec, precision=precise
        )
        entry_factor = jnp.exp(total_log + cumulative) * (seg_b == first_seg).astype(jnp.float32)
        last_seg = seg_b[BLOCK - 1]
        tail_weight = jnp.exp(cumulative[BLOCK - 1] - cumulative + gate_b) * (
            seg_b == last_seg
        ).astype(jnp.float32)
        keep_factor = jnp.exp(cumulative[BLOCK - 1]) * (last_seg == prev_seg).astype(jnp.float32)
        scaled_keys = key_f * tail_weight[:, None]
        cell_state = keep_factor * cell_state + jnp.dot(scaled_keys.T, value_f, precision=precise)
        norm_vec = keep_factor * norm_vec + jnp.sum(scaled_keys, axis=0)
        return (
            (cell_state, norm_vec, last_seg, total_log + cumulative[BLOCK - 1]),
            (numerator, q_norm, entry_factor),
        )

    initial = (
        jnp.zeros((head_dim, column_count), jnp.float32),
        jnp.zeros((head_dim,), jnp.float32),
        first_seg,
        jnp.zeros((), jnp.float32),
    )
    blocks_in = (
        query_all.reshape(block_count, BLOCK, head_dim),
        key_all.reshape(block_count, BLOCK, head_dim),
        value_all.reshape(block_count, BLOCK, column_count),
        gate_in.reshape(block_count, BLOCK),
        log_forget.reshape(block_count, BLOCK),
        segment_ids.reshape(block_count, BLOCK),
    )
    unused, outputs = lax.scan(span_step, initial, blocks_in, unroll=True)
    numerator = outputs[0].reshape(token_count, column_count)
    q_norm = outputs[1].reshape(token_count)
    entry_factor = outputs[2].reshape(token_count)

    linked = (in_last == (first_seg + 1).astype(jnp.float32)).astype(jnp.float32)
    scale_rows = entry_factor * linked
    query_full = query_all.astype(jnp.float32)
    numerator = numerator + scale_rows[:, None] * jnp.dot(query_full, in_state, precision=precise)
    q_norm = q_norm + scale_rows * jnp.dot(query_full, in_norm, precision=precise)
    hidden = (numerator / jnp.maximum(jnp.abs(q_norm), 1.0)[:, None]).astype(jnp.bfloat16)
    returned = lax.all_to_all(
        hidden.reshape(token_count, 1, column_count),
        "tensor",
        split_axis=0,
        concat_axis=1,
        tiled=True,
    )
    hidden_f = returned.astype(jnp.float32).reshape(row_count, head_count, head_dim)
    mean_val = jnp.mean(hidden_f, axis=2, keepdims=True)
    centered = hidden_f - mean_val
    variance = jnp.mean(centered * centered, axis=2, keepdims=True)
    normed = (centered * lax.rsqrt(variance + 1e-05)).reshape(row_count, inner)
    return (normed * norm_gain * jax.nn.silu(output_gate.astype(jnp.float32))).astype(jnp.bfloat16)


def solution(mesh):
    in_specs = (
        P(("seq", "tensor"), None),
        P(("seq", "tensor"), None),
        P(("seq", "tensor"), None),
        P(("seq", "tensor"), None),
        P(("seq", "tensor"), None),
        P("seq"),
        P(("seq", "tensor"), None),
        P(),
    )
    out_specs = P(("seq", "tensor"), None)
    return jax.shard_map(
        on_device, mesh=mesh, in_specs=in_specs, out_specs=out_specs, check_vma=False
    )
```

```python
import math

import jax
import jax.numpy as jnp
from jax import lax
from jax.sharding import PartitionSpec as P

BLOCK = 256


precise = lax.Precision.HIGHEST


def shifted(value, axis, steps):
    count = lax.axis_size(axis)
    initial, last = (max(0, -steps), min(count, count - steps))
    return lax.ppermute(value, axis, [(source, source + steps) for source in range(initial, last)])


def shifted_narrow(value, axis, steps):
    return shifted(value.astype(jnp.bfloat16), axis, steps).astype(jnp.float32)


def meta_row(head_dim, column_count):
    return head_dim + head_dim // column_count


def pack_summary(query_all, key_all, value_all, gate_in, log_forget, segment_ids, key_scale):
    head_dim = key_all.shape[1]
    column_count = value_all.shape[1]
    cumulative = jnp.cumsum(log_forget)
    total_log = cumulative[-1]
    first_seg = segment_ids[0]
    last_seg = segment_ids[-1]
    tail_weight = jnp.exp(total_log - cumulative + gate_in) * (segment_ids == last_seg).astype(
        jnp.float32
    )
    scaled_keys = key_all.astype(jnp.float32) * (key_scale * tail_weight)[:, None]
    state = jnp.dot(scaled_keys.T, value_all.astype(jnp.float32), precision=precise)
    norm = jnp.sum(scaled_keys, axis=0)
    decay = jnp.exp(total_log) * (last_seg == first_seg).astype(jnp.float32)
    norm_rows = head_dim // column_count
    rows = meta_row(head_dim, column_count) + 1
    padded = -(-rows // 8) * 8
    lane = jnp.arange(column_count)
    meta = jnp.where(
        lane == 0,
        decay,
        jnp.where(
            lane == 1,
            (first_seg + 1).astype(jnp.float32),
            jnp.where(lane == 2, (last_seg + 1).astype(jnp.float32), 0.0),
        ),
    )
    filler = jnp.zeros((padded - rows, column_count), jnp.float32)
    return jnp.concatenate(
        [state, norm.reshape(norm_rows, column_count), meta[None, :], filler], axis=0
    )


def combine_packed(earlier, later, head_dim):
    column_count = earlier.shape[1]
    row = meta_row(head_dim, column_count)
    e_decay, e_first, e_last = earlier[row, 0], earlier[row, 1], earlier[row, 2]
    l_decay, l_first, l_last = later[row, 0], later[row, 1], later[row, 2]
    linked = jnp.where((e_last == l_first) | (e_last <= 0.0) | (l_first <= 0.0), 1.0, 0.0)
    factor = jnp.where(l_first <= 0.0, 1.0, l_decay * linked)
    decay_part = jnp.where(e_first <= 0.0, l_decay, e_decay * factor)
    first_seg = jnp.where(e_first <= 0.0, l_first, e_first)
    last_seg = jnp.where(l_last <= 0.0, e_last, l_last)
    body = factor * earlier + later
    lane = jnp.arange(column_count)[None, :]
    rows = jnp.arange(earlier.shape[0])[:, None]
    meta = jnp.where(lane == 0, decay_part, jnp.where(lane == 1, first_seg, last_seg))
    return jnp.where((rows == row) & (lane < 3), meta, body)


def on_device(
    queries, key_rows, values, input_gate, forget_gate, segment_ids, output_gate, norm_gain
):
    tensor_size = lax.axis_size("tensor")
    row_count, inner = queries.shape
    head_count = input_gate.shape[1]
    head_dim = inner // head_count
    group_size = tensor_size // head_count
    column_count = head_dim // group_size

    def spread_heads(array, width):
        shaped = array.reshape(row_count, head_count, 1, width)
        return jnp.broadcast_to(shaped, (row_count, head_count, group_size, width)).reshape(
            row_count, tensor_size, width
        )

    pair_q_k = jnp.stack(
        [
            queries.reshape(row_count, head_count, head_dim),
            key_rows.reshape(row_count, head_count, head_dim),
        ],
        axis=2,
    )
    pair_send = jnp.broadcast_to(
        pair_q_k[:, :, None], (row_count, head_count, group_size // 2, 2, head_dim)
    ).reshape(row_count, tensor_size, head_dim)
    value_send = values.reshape(row_count, tensor_size, column_count)
    both_send = jnp.concatenate([pair_send, value_send], axis=2)
    gate_send = spread_heads(jnp.stack([input_gate, forget_gate], axis=2), 2)
    both_all = lax.all_to_all(both_send, "tensor", split_axis=1, concat_axis=0, tiled=True)
    gate_all = lax.all_to_all(gate_send, "tensor", split_axis=1, concat_axis=0, tiled=True)
    both_all = both_all.reshape(-1, head_dim + column_count)
    own_part = both_all[:, :head_dim]
    value_all = both_all[:, head_dim:]
    other_part = lax.ppermute(
        own_part, "tensor", [(index, index ^ 1) for index in range(tensor_size)]
    )
    is_even = lax.axis_index("tensor") % 2 == 0
    query_all = jnp.where(is_even, own_part, other_part)
    key_all = jnp.where(is_even, other_part, own_part)
    token_count = query_all.shape[0]
    gate_f = gate_all.reshape(token_count, 2).astype(jnp.float32)
    gate_in = gate_f[:, 0]
    log_forget = jax.nn.log_sigmoid(gate_f[:, 1])
    block_count = token_count // BLOCK
    key_scale = 1.0 / math.sqrt(head_dim)
    first_seg = segment_ids[0]

    packed = pack_summary(
        query_all, key_all, value_all, gate_in, log_forget, segment_ids, key_scale
    )
    scanned = packed
    shift = 1
    while shift < lax.axis_size("seq"):
        scanned = combine_packed(shifted_narrow(scanned, "seq", shift), scanned, head_dim)
        shift *= 2
    incoming = shifted_narrow(scanned, "seq", 1)
    in_row = meta_row(head_dim, column_count)
    in_state = incoming[:head_dim]
    in_norm = incoming[head_dim:in_row].reshape(head_dim)
    in_last = incoming[in_row, 2]

    row_ids = jnp.arange(BLOCK, dtype=jnp.int32)
    causal = row_ids[:, None] >= row_ids[None, :]

    def span_step(carry, block_in):
        cell_state, norm_vec, prev_seg, total_log = carry
        query_b, key_b, value_b, gate_b, forget_b, seg_b = block_in
        cumulative = jnp.cumsum(forget_b)
        allowed = causal & (seg_b[:, None] == seg_b[None, :])
        exponent = cumulative[:, None] - cumulative[None, :] + gate_b[None, :]
        weights = jnp.where(allowed, jnp.exp(jnp.where(allowed, exponent, 0.0)), 0.0)
        scores = (
            jnp.einsum("id,jd->ij", query_b, key_b, preferred_element_type=jnp.float32) * key_scale
        )
        weighted = weights * scores
        query_float = query_b.astype(jnp.float32)
        key_f = key_b.astype(jnp.float32) * key_scale
        value_f = value_b.astype(jnp.float32)
        numerator = jnp.dot(weighted, value_f, precision=precise)
        carried = jnp.exp(cumulative) * (seg_b == prev_seg).astype(jnp.float32)
        numerator = numerator + carried[:, None] * jnp.dot(
            query_float, cell_state, precision=precise
        )
        q_norm = jnp.sum(weighted, axis=1) + carried * jnp.dot(
            query_float, norm_vec, precision=precise
        )
        entry_factor = jnp.exp(total_log + cumulative) * (seg_b == first_seg).astype(jnp.float32)
        last_seg = seg_b[BLOCK - 1]
        tail_weight = jnp.exp(cumulative[BLOCK - 1] - cumulative + gate_b) * (
            seg_b == last_seg
        ).astype(jnp.float32)
        keep_factor = jnp.exp(cumulative[BLOCK - 1]) * (last_seg == prev_seg).astype(jnp.float32)
        scaled_keys = key_f * tail_weight[:, None]
        cell_state = keep_factor * cell_state + jnp.dot(scaled_keys.T, value_f, precision=precise)
        norm_vec = keep_factor * norm_vec + jnp.sum(scaled_keys, axis=0)
        return (
            (cell_state, norm_vec, last_seg, total_log + cumulative[BLOCK - 1]),
            (numerator, q_norm, entry_factor),
        )

    initial = (
        jnp.zeros((head_dim, column_count), jnp.float32),
        jnp.zeros((head_dim,), jnp.float32),
        first_seg,
        jnp.zeros((), jnp.float32),
    )
    blocks_in = (
        query_all.reshape(block_count, BLOCK, head_dim),
        key_all.reshape(block_count, BLOCK, head_dim),
        value_all.reshape(block_count, BLOCK, column_count),
        gate_in.reshape(block_count, BLOCK),
        log_forget.reshape(block_count, BLOCK),
        segment_ids.reshape(block_count, BLOCK),
    )
    unused, outputs = lax.scan(span_step, initial, blocks_in, unroll=True)
    numerator = outputs[0].reshape(token_count, column_count)
    q_norm = outputs[1].reshape(token_count)
    entry_factor = outputs[2].reshape(token_count)

    linked = (in_last == (first_seg + 1).astype(jnp.float32)).astype(jnp.float32)
    scale_rows = entry_factor * linked
    query_full = query_all.astype(jnp.float32)
    numerator = numerator + scale_rows[:, None] * jnp.dot(query_full, in_state, precision=precise)
    q_norm = q_norm + scale_rows * jnp.dot(query_full, in_norm, precision=precise)
    hidden = (numerator / jnp.maximum(jnp.abs(q_norm), 1.0)[:, None]).astype(jnp.bfloat16)
    returned = lax.all_to_all(
        hidden.reshape(token_count, 1, column_count),
        "tensor",
        split_axis=0,
        concat_axis=1,
        tiled=True,
    )
    hidden_f = returned.astype(jnp.float32).reshape(row_count, head_count, head_dim)
    mean_val = jnp.mean(hidden_f, axis=2, keepdims=True)
    centered = hidden_f - mean_val
    variance = jnp.mean(centered * centered, axis=2, keepdims=True)
    normed = (centered * lax.rsqrt(variance + 1e-05)).reshape(row_count, inner)
    return (normed * norm_gain * jax.nn.silu(output_gate.astype(jnp.float32))).astype(jnp.bfloat16)


def solution(mesh):
    in_specs = (
        P(("seq", "tensor"), None),
        P(("seq", "tensor"), None),
        P(("seq", "tensor"), None),
        P(("seq", "tensor"), None),
        P(("seq", "tensor"), None),
        P("seq"),
        P(("seq", "tensor"), None),
        P(),
    )
    out_specs = P(("seq", "tensor"), None)
    return jax.shard_map(
        on_device, mesh=mesh, in_specs=in_specs, out_specs=out_specs, check_vma=False
    )
```

```python
import math

import jax
import jax.numpy as jnp
from jax import lax
from jax.sharding import PartitionSpec as P

BLOCK = 256


precise = lax.Precision.HIGHEST


def shifted(value, axis, steps):
    count = lax.axis_size(axis)
    initial, last = (max(0, -steps), min(count, count - steps))
    return lax.ppermute(value, axis, [(source, source + steps) for source in range(initial, last)])


def shifted_narrow(value, axis, steps):
    return shifted(value.astype(jnp.bfloat16), axis, steps).astype(jnp.float32)


def meta_row(head_dim, column_count):
    return head_dim + head_dim // column_count


def pack_summary(query_all, key_all, value_all, gate_in, log_forget, segment_ids, key_scale):
    head_dim = key_all.shape[1]
    column_count = value_all.shape[1]
    cumulative = jnp.cumsum(log_forget)
    total_log = cumulative[-1]
    first_seg = segment_ids[0]
    last_seg = segment_ids[-1]
    tail_weight = jnp.exp(total_log - cumulative + gate_in) * (segment_ids == last_seg).astype(
        jnp.float32
    )
    scaled_keys = key_all.astype(jnp.float32) * (key_scale * tail_weight)[:, None]
    state = jnp.dot(scaled_keys.T, value_all.astype(jnp.float32), precision=precise)
    norm = jnp.sum(scaled_keys, axis=0)
    decay = jnp.exp(total_log) * (last_seg == first_seg).astype(jnp.float32)
    norm_rows = head_dim // column_count
    rows = meta_row(head_dim, column_count) + 1
    padded = -(-rows // 8) * 8
    lane = jnp.arange(column_count)
    meta = jnp.where(
        lane == 0,
        decay,
        jnp.where(
            lane == 1,
            (first_seg + 1).astype(jnp.float32),
            jnp.where(lane == 2, (last_seg + 1).astype(jnp.float32), 0.0),
        ),
    )
    filler = jnp.zeros((padded - rows, column_count), jnp.float32)
    return jnp.concatenate(
        [state, norm.reshape(norm_rows, column_count), meta[None, :], filler], axis=0
    )


def combine_packed(earlier, later, head_dim):
    column_count = earlier.shape[1]
    row = meta_row(head_dim, column_count)
    e_decay, e_first, e_last = earlier[row, 0], earlier[row, 1], earlier[row, 2]
    l_decay, l_first, l_last = later[row, 0], later[row, 1], later[row, 2]
    linked = jnp.where((e_last == l_first) | (e_last <= 0.0) | (l_first <= 0.0), 1.0, 0.0)
    factor = jnp.where(l_first <= 0.0, 1.0, l_decay * linked)
    decay_part = jnp.where(e_first <= 0.0, l_decay, e_decay * factor)
    first_seg = jnp.where(e_first <= 0.0, l_first, e_first)
    last_seg = jnp.where(l_last <= 0.0, e_last, l_last)
    body = factor * earlier + later
    lane = jnp.arange(column_count)[None, :]
    rows = jnp.arange(earlier.shape[0])[:, None]
    meta = jnp.where(lane == 0, decay_part, jnp.where(lane == 1, first_seg, last_seg))
    return jnp.where((rows == row) & (lane < 3), meta, body)


def prefix_from_all(packed, head_dim):
    seq_count = lax.axis_size("seq")
    column_count = packed.shape[1]
    row = meta_row(head_dim, column_count)
    gathered = lax.all_gather(packed.astype(jnp.bfloat16), "seq")
    meta = lax.all_gather(packed[row, :8], "seq")
    decay, first, last = meta[:, 0], meta[:, 1], meta[:, 2]
    me = lax.axis_index("seq")
    order = jnp.arange(seq_count)
    previous_last = jnp.concatenate([jnp.zeros((1,), jnp.float32), last[:-1]])
    carry = decay * (previous_last == first).astype(jnp.float32)
    carry = jnp.where(order < me, carry, 1.0)
    after = jnp.cumprod(carry[::-1])[::-1]
    weight = jnp.concatenate([after[1:], jnp.ones((1,), jnp.float32)])
    weight = jnp.where(order < me, weight, 0.0)
    total = jnp.einsum("s,src->rc", weight, gathered.astype(jnp.float32))
    in_last = jnp.where(me > 0, last[jnp.maximum(me - 1, 0)], 0.0)
    lane = jnp.arange(column_count)[None, :]
    rows = jnp.arange(packed.shape[0])[:, None]
    return jnp.where((rows == row) & (lane == 2), in_last, total)


def on_device(
    queries, key_rows, values, input_gate, forget_gate, segment_ids, output_gate, norm_gain
):
    tensor_size = lax.axis_size("tensor")
    row_count, inner = queries.shape
    head_count = input_gate.shape[1]
    head_dim = inner // head_count
    group_size = tensor_size // head_count
    column_count = head_dim // group_size

    def spread_heads(array, width):
        shaped = array.reshape(row_count, head_count, 1, width)
        return jnp.broadcast_to(shaped, (row_count, head_count, group_size, width)).reshape(
            row_count, tensor_size, width
        )

    pair_q_k = jnp.stack(
        [
            queries.reshape(row_count, head_count, head_dim),
            key_rows.reshape(row_count, head_count, head_dim),
        ],
        axis=2,
    )
    pair_send = jnp.broadcast_to(
        pair_q_k[:, :, None], (row_count, head_count, group_size // 2, 2, head_dim)
    ).reshape(row_count, tensor_size, head_dim)
    value_send = values.reshape(row_count, tensor_size, column_count)
    both_send = jnp.concatenate([pair_send, value_send], axis=2)
    gate_send = spread_heads(jnp.stack([input_gate, forget_gate], axis=2), 2)
    both_all = lax.all_to_all(both_send, "tensor", split_axis=1, concat_axis=0, tiled=True)
    gate_all = lax.all_to_all(gate_send, "tensor", split_axis=1, concat_axis=0, tiled=True)
    both_all = both_all.reshape(-1, head_dim + column_count)
    own_part = both_all[:, :head_dim]
    value_all = both_all[:, head_dim:]
    other_part = lax.ppermute(
        own_part, "tensor", [(index, index ^ 1) for index in range(tensor_size)]
    )
    is_even = lax.axis_index("tensor") % 2 == 0
    query_all = jnp.where(is_even, own_part, other_part)
    key_all = jnp.where(is_even, other_part, own_part)
    token_count = query_all.shape[0]
    gate_f = gate_all.reshape(token_count, 2).astype(jnp.float32)
    gate_in = gate_f[:, 0]
    log_forget = jax.nn.log_sigmoid(gate_f[:, 1])
    block_count = token_count // BLOCK
    key_scale = 1.0 / math.sqrt(head_dim)
    first_seg = segment_ids[0]

    packed = pack_summary(
        query_all, key_all, value_all, gate_in, log_forget, segment_ids, key_scale
    )
    incoming = prefix_from_all(packed, head_dim)
    in_row = meta_row(head_dim, column_count)
    in_state = incoming[:head_dim]
    in_norm = incoming[head_dim:in_row].reshape(head_dim)
    in_last = incoming[in_row, 2]

    row_ids = jnp.arange(BLOCK, dtype=jnp.int32)
    causal = row_ids[:, None] >= row_ids[None, :]

    def span_step(carry, block_in):
        cell_state, norm_vec, prev_seg, total_log = carry
        query_b, key_b, value_b, gate_b, forget_b, seg_b = block_in
        cumulative = jnp.cumsum(forget_b)
        allowed = causal & (seg_b[:, None] == seg_b[None, :])
        exponent = cumulative[:, None] - cumulative[None, :] + gate_b[None, :]
        weights = jnp.where(allowed, jnp.exp(jnp.where(allowed, exponent, 0.0)), 0.0)
        scores = (
            jnp.einsum("id,jd->ij", query_b, key_b, preferred_element_type=jnp.float32) * key_scale
        )
        weighted = weights * scores
        query_float = query_b.astype(jnp.float32)
        key_f = key_b.astype(jnp.float32) * key_scale
        value_f = value_b.astype(jnp.float32)
        numerator = jnp.dot(weighted, value_f, precision=precise)
        carried = jnp.exp(cumulative) * (seg_b == prev_seg).astype(jnp.float32)
        numerator = numerator + carried[:, None] * jnp.dot(
            query_float, cell_state, precision=precise
        )
        q_norm = jnp.sum(weighted, axis=1) + carried * jnp.dot(
            query_float, norm_vec, precision=precise
        )
        entry_factor = jnp.exp(total_log + cumulative) * (seg_b == first_seg).astype(jnp.float32)
        last_seg = seg_b[BLOCK - 1]
        tail_weight = jnp.exp(cumulative[BLOCK - 1] - cumulative + gate_b) * (
            seg_b == last_seg
        ).astype(jnp.float32)
        keep_factor = jnp.exp(cumulative[BLOCK - 1]) * (last_seg == prev_seg).astype(jnp.float32)
        scaled_keys = key_f * tail_weight[:, None]
        cell_state = keep_factor * cell_state + jnp.dot(scaled_keys.T, value_f, precision=precise)
        norm_vec = keep_factor * norm_vec + jnp.sum(scaled_keys, axis=0)
        return (
            (cell_state, norm_vec, last_seg, total_log + cumulative[BLOCK - 1]),
            (numerator, q_norm, entry_factor),
        )

    initial = (
        jnp.zeros((head_dim, column_count), jnp.float32),
        jnp.zeros((head_dim,), jnp.float32),
        first_seg,
        jnp.zeros((), jnp.float32),
    )
    blocks_in = (
        query_all.reshape(block_count, BLOCK, head_dim),
        key_all.reshape(block_count, BLOCK, head_dim),
        value_all.reshape(block_count, BLOCK, column_count),
        gate_in.reshape(block_count, BLOCK),
        log_forget.reshape(block_count, BLOCK),
        segment_ids.reshape(block_count, BLOCK),
    )
    unused, outputs = lax.scan(span_step, initial, blocks_in, unroll=True)
    numerator = outputs[0].reshape(token_count, column_count)
    q_norm = outputs[1].reshape(token_count)
    entry_factor = outputs[2].reshape(token_count)

    linked = (in_last == (first_seg + 1).astype(jnp.float32)).astype(jnp.float32)
    scale_rows = entry_factor * linked
    query_full = query_all.astype(jnp.float32)
    numerator = numerator + scale_rows[:, None] * jnp.dot(query_full, in_state, precision=precise)
    q_norm = q_norm + scale_rows * jnp.dot(query_full, in_norm, precision=precise)
    hidden = (numerator / jnp.maximum(jnp.abs(q_norm), 1.0)[:, None]).astype(jnp.bfloat16)
    returned = lax.all_to_all(
        hidden.reshape(token_count, 1, column_count),
        "tensor",
        split_axis=0,
        concat_axis=1,
        tiled=True,
    )
    hidden_f = returned.astype(jnp.float32).reshape(row_count, head_count, head_dim)
    mean_val = jnp.mean(hidden_f, axis=2, keepdims=True)
    centered = hidden_f - mean_val
    variance = jnp.mean(centered * centered, axis=2, keepdims=True)
    normed = (centered * lax.rsqrt(variance + 1e-05)).reshape(row_count, inner)
    return (normed * norm_gain * jax.nn.silu(output_gate.astype(jnp.float32))).astype(jnp.bfloat16)


def solution(mesh):
    in_specs = (
        P(("seq", "tensor"), None),
        P(("seq", "tensor"), None),
        P(("seq", "tensor"), None),
        P(("seq", "tensor"), None),
        P(("seq", "tensor"), None),
        P("seq"),
        P(("seq", "tensor"), None),
        P(),
    )
    out_specs = P(("seq", "tensor"), None)
    return jax.shard_map(
        on_device, mesh=mesh, in_specs=in_specs, out_specs=out_specs, check_vma=False
    )
```

```python
import math

import jax
import jax.numpy as jnp
from jax import lax
from jax.sharding import PartitionSpec as P

BLOCK = 256


precise = lax.Precision.HIGHEST


def shifted(value, axis, steps):
    count = lax.axis_size(axis)
    initial, last = (max(0, -steps), min(count, count - steps))
    return lax.ppermute(value, axis, [(source, source + steps) for source in range(initial, last)])


def shifted_narrow(value, axis, steps):
    return shifted(value.astype(jnp.bfloat16), axis, steps).astype(jnp.float32)


def meta_row(head_dim, column_count):
    return head_dim + head_dim // column_count


def pack_summary(query_all, key_all, value_all, gate_in, log_forget, segment_ids, key_scale):
    head_dim = key_all.shape[1]
    column_count = value_all.shape[1]
    cumulative = jnp.cumsum(log_forget)
    total_log = cumulative[-1]
    first_seg = segment_ids[0]
    last_seg = segment_ids[-1]
    tail_weight = jnp.exp(total_log - cumulative + gate_in) * (segment_ids == last_seg).astype(
        jnp.float32
    )
    scaled_keys = key_all.astype(jnp.float32) * (key_scale * tail_weight)[:, None]
    state = jnp.dot(scaled_keys.T, value_all.astype(jnp.float32), precision=precise)
    norm = jnp.sum(scaled_keys, axis=0)
    decay = jnp.exp(total_log) * (last_seg == first_seg).astype(jnp.float32)
    norm_rows = head_dim // column_count
    rows = meta_row(head_dim, column_count) + 1
    padded = -(-rows // 8) * 8
    lane = jnp.arange(column_count)
    decay_high = lax.reduce_precision(decay, exponent_bits=8, mantissa_bits=7)
    meta = jnp.where(
        lane == 0,
        decay_high,
        jnp.where(
            lane == 1,
            (first_seg + 1).astype(jnp.float32),
            jnp.where(
                lane == 2,
                (last_seg + 1).astype(jnp.float32),
                jnp.where(lane == 3, decay - decay_high, 0.0),
            ),
        ),
    )
    filler = jnp.zeros((padded - rows, column_count), jnp.float32)
    return jnp.concatenate(
        [state, norm.reshape(norm_rows, column_count), meta[None, :], filler], axis=0
    )


def combine_packed(earlier, later, head_dim):
    column_count = earlier.shape[1]
    row = meta_row(head_dim, column_count)
    e_decay, e_first, e_last = earlier[row, 0], earlier[row, 1], earlier[row, 2]
    l_decay, l_first, l_last = later[row, 0], later[row, 1], later[row, 2]
    linked = jnp.where((e_last == l_first) | (e_last <= 0.0) | (l_first <= 0.0), 1.0, 0.0)
    factor = jnp.where(l_first <= 0.0, 1.0, l_decay * linked)
    decay_part = jnp.where(e_first <= 0.0, l_decay, e_decay * factor)
    first_seg = jnp.where(e_first <= 0.0, l_first, e_first)
    last_seg = jnp.where(l_last <= 0.0, e_last, l_last)
    body = factor * earlier + later
    lane = jnp.arange(column_count)[None, :]
    rows = jnp.arange(earlier.shape[0])[:, None]
    meta = jnp.where(lane == 0, decay_part, jnp.where(lane == 1, first_seg, last_seg))
    return jnp.where((rows == row) & (lane < 3), meta, body)


def prefix_from_all(packed, head_dim):
    seq_count = lax.axis_size("seq")
    column_count = packed.shape[1]
    row = meta_row(head_dim, column_count)
    gathered = lax.all_gather(packed.astype(jnp.bfloat16), "seq")
    meta = gathered[:, row, :8].astype(jnp.float32)
    decay, first, last = meta[:, 0] + meta[:, 3], meta[:, 1], meta[:, 2]
    me = lax.axis_index("seq")
    order = jnp.arange(seq_count)
    previous_last = jnp.concatenate([jnp.zeros((1,), jnp.float32), last[:-1]])
    carry = decay * (previous_last == first).astype(jnp.float32)
    carry = jnp.where(order < me, carry, 1.0)
    after = jnp.cumprod(carry[::-1])[::-1]
    weight = jnp.concatenate([after[1:], jnp.ones((1,), jnp.float32)])
    weight = jnp.where(order < me, weight, 0.0)
    total = jnp.einsum("s,src->rc", weight, gathered.astype(jnp.float32))
    in_last = jnp.where(me > 0, last[jnp.maximum(me - 1, 0)], 0.0)
    lane = jnp.arange(column_count)[None, :]
    rows = jnp.arange(packed.shape[0])[:, None]
    return jnp.where((rows == row) & (lane == 2), in_last, total)


def on_device(
    queries, key_rows, values, input_gate, forget_gate, segment_ids, output_gate, norm_gain
):
    tensor_size = lax.axis_size("tensor")
    row_count, inner = queries.shape
    head_count = input_gate.shape[1]
    head_dim = inner // head_count
    group_size = tensor_size // head_count
    column_count = head_dim // group_size

    def spread_heads(array, width):
        shaped = array.reshape(row_count, head_count, 1, width)
        return jnp.broadcast_to(shaped, (row_count, head_count, group_size, width)).reshape(
            row_count, tensor_size, width
        )

    pair_q_k = jnp.stack(
        [
            queries.reshape(row_count, head_count, head_dim),
            key_rows.reshape(row_count, head_count, head_dim),
        ],
        axis=2,
    )
    pair_send = jnp.broadcast_to(
        pair_q_k[:, :, None], (row_count, head_count, group_size // 2, 2, head_dim)
    ).reshape(row_count, tensor_size, head_dim)
    value_send = values.reshape(row_count, tensor_size, column_count)
    both_send = jnp.concatenate([pair_send, value_send], axis=2)
    gate_send = spread_heads(jnp.stack([input_gate, forget_gate], axis=2), 2)
    both_all = lax.all_to_all(both_send, "tensor", split_axis=1, concat_axis=0, tiled=True)
    gate_all = lax.all_to_all(gate_send, "tensor", split_axis=1, concat_axis=0, tiled=True)
    both_all = both_all.reshape(-1, head_dim + column_count)
    own_part = both_all[:, :head_dim]
    value_all = both_all[:, head_dim:]
    other_part = lax.ppermute(
        own_part, "tensor", [(index, index ^ 1) for index in range(tensor_size)]
    )
    is_even = lax.axis_index("tensor") % 2 == 0
    query_all = jnp.where(is_even, own_part, other_part)
    key_all = jnp.where(is_even, other_part, own_part)
    token_count = query_all.shape[0]
    gate_f = gate_all.reshape(token_count, 2).astype(jnp.float32)
    gate_in = gate_f[:, 0]
    log_forget = jax.nn.log_sigmoid(gate_f[:, 1])
    block_count = token_count // BLOCK
    key_scale = 1.0 / math.sqrt(head_dim)
    first_seg = segment_ids[0]

    packed = pack_summary(
        query_all, key_all, value_all, gate_in, log_forget, segment_ids, key_scale
    )
    incoming = prefix_from_all(packed, head_dim)
    in_row = meta_row(head_dim, column_count)
    in_state = incoming[:head_dim]
    in_norm = incoming[head_dim:in_row].reshape(head_dim)
    in_last = incoming[in_row, 2]

    row_ids = jnp.arange(BLOCK, dtype=jnp.int32)
    causal = row_ids[:, None] >= row_ids[None, :]

    def span_step(carry, block_in):
        cell_state, norm_vec, prev_seg, total_log = carry
        query_b, key_b, value_b, gate_b, forget_b, seg_b = block_in
        cumulative = jnp.cumsum(forget_b)
        allowed = causal & (seg_b[:, None] == seg_b[None, :])
        exponent = cumulative[:, None] - cumulative[None, :] + gate_b[None, :]
        weights = jnp.where(allowed, jnp.exp(jnp.where(allowed, exponent, 0.0)), 0.0)
        scores = (
            jnp.einsum("id,jd->ij", query_b, key_b, preferred_element_type=jnp.float32) * key_scale
        )
        weighted = weights * scores
        query_float = query_b.astype(jnp.float32)
        key_f = key_b.astype(jnp.float32) * key_scale
        value_f = value_b.astype(jnp.float32)
        numerator = jnp.dot(weighted, value_f, precision=precise)
        carried = jnp.exp(cumulative) * (seg_b == prev_seg).astype(jnp.float32)
        numerator = numerator + carried[:, None] * jnp.dot(
            query_float, cell_state, precision=precise
        )
        q_norm = jnp.sum(weighted, axis=1) + carried * jnp.dot(
            query_float, norm_vec, precision=precise
        )
        entry_factor = jnp.exp(total_log + cumulative) * (seg_b == first_seg).astype(jnp.float32)
        last_seg = seg_b[BLOCK - 1]
        tail_weight = jnp.exp(cumulative[BLOCK - 1] - cumulative + gate_b) * (
            seg_b == last_seg
        ).astype(jnp.float32)
        keep_factor = jnp.exp(cumulative[BLOCK - 1]) * (last_seg == prev_seg).astype(jnp.float32)
        scaled_keys = key_f * tail_weight[:, None]
        cell_state = keep_factor * cell_state + jnp.dot(scaled_keys.T, value_f, precision=precise)
        norm_vec = keep_factor * norm_vec + jnp.sum(scaled_keys, axis=0)
        return (
            (cell_state, norm_vec, last_seg, total_log + cumulative[BLOCK - 1]),
            (numerator, q_norm, entry_factor),
        )

    initial = (
        jnp.zeros((head_dim, column_count), jnp.float32),
        jnp.zeros((head_dim,), jnp.float32),
        first_seg,
        jnp.zeros((), jnp.float32),
    )
    blocks_in = (
        query_all.reshape(block_count, BLOCK, head_dim),
        key_all.reshape(block_count, BLOCK, head_dim),
        value_all.reshape(block_count, BLOCK, column_count),
        gate_in.reshape(block_count, BLOCK),
        log_forget.reshape(block_count, BLOCK),
        segment_ids.reshape(block_count, BLOCK),
    )
    unused, outputs = lax.scan(span_step, initial, blocks_in, unroll=True)
    numerator = outputs[0].reshape(token_count, column_count)
    q_norm = outputs[1].reshape(token_count)
    entry_factor = outputs[2].reshape(token_count)

    linked = (in_last == (first_seg + 1).astype(jnp.float32)).astype(jnp.float32)
    scale_rows = entry_factor * linked
    query_full = query_all.astype(jnp.float32)
    numerator = numerator + scale_rows[:, None] * jnp.dot(query_full, in_state, precision=precise)
    q_norm = q_norm + scale_rows * jnp.dot(query_full, in_norm, precision=precise)
    hidden = (numerator / jnp.maximum(jnp.abs(q_norm), 1.0)[:, None]).astype(jnp.bfloat16)
    returned = lax.all_to_all(
        hidden.reshape(token_count, 1, column_count),
        "tensor",
        split_axis=0,
        concat_axis=1,
        tiled=True,
    )
    hidden_f = returned.astype(jnp.float32).reshape(row_count, head_count, head_dim)
    mean_val = jnp.mean(hidden_f, axis=2, keepdims=True)
    centered = hidden_f - mean_val
    variance = jnp.mean(centered * centered, axis=2, keepdims=True)
    normed = (centered * lax.rsqrt(variance + 1e-05)).reshape(row_count, inner)
    return (normed * norm_gain * jax.nn.silu(output_gate.astype(jnp.float32))).astype(jnp.bfloat16)


def solution(mesh):
    in_specs = (
        P(("seq", "tensor"), None),
        P(("seq", "tensor"), None),
        P(("seq", "tensor"), None),
        P(("seq", "tensor"), None),
        P(("seq", "tensor"), None),
        P("seq"),
        P(("seq", "tensor"), None),
        P(),
    )
    out_specs = P(("seq", "tensor"), None)
    return jax.shard_map(
        on_device, mesh=mesh, in_specs=in_specs, out_specs=out_specs, check_vma=False
    )
```

```python
import math

import jax
import jax.numpy as jnp
from jax import lax
from jax.sharding import PartitionSpec as P

BLOCK = 256


precise = lax.Precision.HIGHEST


def shifted(value, axis, steps):
    count = lax.axis_size(axis)
    initial, last = (max(0, -steps), min(count, count - steps))
    return lax.ppermute(value, axis, [(source, source + steps) for source in range(initial, last)])


def shifted_narrow(value, axis, steps):
    return shifted(value.astype(jnp.bfloat16), axis, steps).astype(jnp.float32)


def meta_row(head_dim, column_count):
    return head_dim + head_dim // column_count


def pack_summary(query_all, key_all, value_all, gate_in, log_forget, segment_ids, key_scale):
    head_dim = key_all.shape[1]
    column_count = value_all.shape[1]
    cumulative = jnp.cumsum(log_forget)
    total_log = cumulative[-1]
    first_seg = segment_ids[0]
    last_seg = segment_ids[-1]
    tail_weight = jnp.exp(total_log - cumulative + gate_in) * (segment_ids == last_seg).astype(
        jnp.float32
    )
    scaled_keys = key_all.astype(jnp.float32) * (key_scale * tail_weight)[:, None]
    state = jnp.dot(scaled_keys.T, value_all.astype(jnp.float32), precision=precise)
    norm = jnp.sum(scaled_keys, axis=0)
    decay = jnp.exp(total_log) * (last_seg == first_seg).astype(jnp.float32)
    norm_rows = head_dim // column_count
    rows = meta_row(head_dim, column_count) + 1
    padded = -(-rows // 8) * 8
    lane = jnp.arange(column_count)
    decay_high = lax.reduce_precision(decay, exponent_bits=8, mantissa_bits=7)
    meta = jnp.where(
        lane == 0,
        decay_high,
        jnp.where(
            lane == 1,
            (first_seg + 1).astype(jnp.float32),
            jnp.where(
                lane == 2,
                (last_seg + 1).astype(jnp.float32),
                jnp.where(lane == 3, decay - decay_high, 0.0),
            ),
        ),
    )
    filler = jnp.zeros((padded - rows, column_count), jnp.float32)
    return jnp.concatenate(
        [state, norm.reshape(norm_rows, column_count), meta[None, :], filler], axis=0
    )


def combine_packed(earlier, later, head_dim):
    column_count = earlier.shape[1]
    row = meta_row(head_dim, column_count)
    e_decay, e_first, e_last = earlier[row, 0], earlier[row, 1], earlier[row, 2]
    l_decay, l_first, l_last = later[row, 0], later[row, 1], later[row, 2]
    linked = jnp.where((e_last == l_first) | (e_last <= 0.0) | (l_first <= 0.0), 1.0, 0.0)
    factor = jnp.where(l_first <= 0.0, 1.0, l_decay * linked)
    decay_part = jnp.where(e_first <= 0.0, l_decay, e_decay * factor)
    first_seg = jnp.where(e_first <= 0.0, l_first, e_first)
    last_seg = jnp.where(l_last <= 0.0, e_last, l_last)
    body = factor * earlier + later
    lane = jnp.arange(column_count)[None, :]
    rows = jnp.arange(earlier.shape[0])[:, None]
    meta = jnp.where(lane == 0, decay_part, jnp.where(lane == 1, first_seg, last_seg))
    return jnp.where((rows == row) & (lane < 3), meta, body)


def prefix_from_all(packed, head_dim):
    seq_count = lax.axis_size("seq")
    column_count = packed.shape[1]
    row = meta_row(head_dim, column_count)
    gathered = lax.all_gather(packed.astype(jnp.bfloat16), "seq")
    meta = gathered[:, row, :8].astype(jnp.float32)
    decay, first, last = meta[:, 0] + meta[:, 3], meta[:, 1], meta[:, 2]
    me = lax.axis_index("seq")
    order = jnp.arange(seq_count)
    previous_last = jnp.concatenate([jnp.zeros((1,), jnp.float32), last[:-1]])
    carry = decay * (previous_last == first).astype(jnp.float32)
    carry = jnp.where(order < me, carry, 1.0)
    after = jnp.cumprod(carry[::-1])[::-1]
    weight = jnp.concatenate([after[1:], jnp.ones((1,), jnp.float32)])
    weight = jnp.where(order < me, weight, 0.0)
    total = jnp.einsum("s,src->rc", weight, gathered.astype(jnp.float32))
    in_last = jnp.where(me > 0, last[jnp.maximum(me - 1, 0)], 0.0)
    lane = jnp.arange(column_count)[None, :]
    rows = jnp.arange(packed.shape[0])[:, None]
    return jnp.where((rows == row) & (lane == 2), in_last, total)


def on_device(
    queries, key_rows, values, input_gate, forget_gate, segment_ids, output_gate, norm_gain
):
    tensor_size = lax.axis_size("tensor")
    row_count, inner = queries.shape
    head_count = input_gate.shape[1]
    head_dim = inner // head_count
    group_size = tensor_size // head_count
    column_count = head_dim // group_size

    def spread_heads(array, width):
        shaped = array.reshape(row_count, head_count, 1, width)
        return jnp.broadcast_to(shaped, (row_count, head_count, group_size, width)).reshape(
            row_count, tensor_size, width
        )

    pair_q_k = jnp.stack(
        [
            queries.reshape(row_count, head_count, head_dim),
            key_rows.reshape(row_count, head_count, head_dim),
        ],
        axis=2,
    )
    pair_send = jnp.broadcast_to(
        pair_q_k[:, :, None], (row_count, head_count, group_size // 2, 2, head_dim)
    ).reshape(row_count, tensor_size, head_dim)
    value_send = values.reshape(row_count, tensor_size, column_count)
    both_send = jnp.concatenate([pair_send, value_send], axis=2)
    both_all = lax.all_to_all(both_send, "tensor", split_axis=1, concat_axis=0, tiled=True)
    gate_every = lax.all_gather(jnp.stack([input_gate, forget_gate], axis=0), "tensor", axis=1, tiled=True)
    my_head = lax.axis_index("tensor") // group_size
    gate_all = lax.dynamic_index_in_dim(gate_every, my_head, axis=2, keepdims=False)
    both_all = both_all.reshape(-1, head_dim + column_count)
    own_part = both_all[:, :head_dim]
    value_all = both_all[:, head_dim:]
    other_part = lax.ppermute(
        own_part, "tensor", [(index, index ^ 1) for index in range(tensor_size)]
    )
    is_even = lax.axis_index("tensor") % 2 == 0
    query_all = jnp.where(is_even, own_part, other_part)
    key_all = jnp.where(is_even, other_part, own_part)
    token_count = query_all.shape[0]
    gate_f = gate_all.astype(jnp.float32)
    gate_in = gate_f[0]
    log_forget = jax.nn.log_sigmoid(gate_f[1])
    block_count = token_count // BLOCK
    key_scale = 1.0 / math.sqrt(head_dim)
    first_seg = segment_ids[0]

    packed = pack_summary(
        query_all, key_all, value_all, gate_in, log_forget, segment_ids, key_scale
    )
    incoming = prefix_from_all(packed, head_dim)
    in_row = meta_row(head_dim, column_count)
    in_state = incoming[:head_dim]
    in_norm = incoming[head_dim:in_row].reshape(head_dim)
    in_last = incoming[in_row, 2]

    row_ids = jnp.arange(BLOCK, dtype=jnp.int32)
    causal = row_ids[:, None] >= row_ids[None, :]

    def span_step(carry, block_in):
        cell_state, norm_vec, prev_seg, total_log = carry
        query_b, key_b, value_b, gate_b, forget_b, seg_b = block_in
        cumulative = jnp.cumsum(forget_b)
        allowed = causal & (seg_b[:, None] == seg_b[None, :])
        exponent = cumulative[:, None] - cumulative[None, :] + gate_b[None, :]
        weights = jnp.where(allowed, jnp.exp(jnp.where(allowed, exponent, 0.0)), 0.0)
        scores = (
            jnp.einsum("id,jd->ij", query_b, key_b, preferred_element_type=jnp.float32) * key_scale
        )
        weighted = weights * scores
        query_float = query_b.astype(jnp.float32)
        key_f = key_b.astype(jnp.float32) * key_scale
        value_f = value_b.astype(jnp.float32)
        numerator = jnp.dot(weighted, value_f, precision=precise)
        carried = jnp.exp(cumulative) * (seg_b == prev_seg).astype(jnp.float32)
        numerator = numerator + carried[:, None] * jnp.dot(
            query_float, cell_state, precision=precise
        )
        q_norm = jnp.sum(weighted, axis=1) + carried * jnp.dot(
            query_float, norm_vec, precision=precise
        )
        entry_factor = jnp.exp(total_log + cumulative) * (seg_b == first_seg).astype(jnp.float32)
        last_seg = seg_b[BLOCK - 1]
        tail_weight = jnp.exp(cumulative[BLOCK - 1] - cumulative + gate_b) * (
            seg_b == last_seg
        ).astype(jnp.float32)
        keep_factor = jnp.exp(cumulative[BLOCK - 1]) * (last_seg == prev_seg).astype(jnp.float32)
        scaled_keys = key_f * tail_weight[:, None]
        cell_state = keep_factor * cell_state + jnp.dot(scaled_keys.T, value_f, precision=precise)
        norm_vec = keep_factor * norm_vec + jnp.sum(scaled_keys, axis=0)
        return (
            (cell_state, norm_vec, last_seg, total_log + cumulative[BLOCK - 1]),
            (numerator, q_norm, entry_factor),
        )

    initial = (
        jnp.zeros((head_dim, column_count), jnp.float32),
        jnp.zeros((head_dim,), jnp.float32),
        first_seg,
        jnp.zeros((), jnp.float32),
    )
    blocks_in = (
        query_all.reshape(block_count, BLOCK, head_dim),
        key_all.reshape(block_count, BLOCK, head_dim),
        value_all.reshape(block_count, BLOCK, column_count),
        gate_in.reshape(block_count, BLOCK),
        log_forget.reshape(block_count, BLOCK),
        segment_ids.reshape(block_count, BLOCK),
    )
    unused, outputs = lax.scan(span_step, initial, blocks_in)
    numerator = outputs[0].reshape(token_count, column_count)
    q_norm = outputs[1].reshape(token_count)
    entry_factor = outputs[2].reshape(token_count)

    linked = (in_last == (first_seg + 1).astype(jnp.float32)).astype(jnp.float32)
    scale_rows = entry_factor * linked
    query_full = query_all.astype(jnp.float32)
    numerator = numerator + scale_rows[:, None] * jnp.dot(query_full, in_state, precision=precise)
    q_norm = q_norm + scale_rows * jnp.dot(query_full, in_norm, precision=precise)
    hidden = (numerator / jnp.maximum(jnp.abs(q_norm), 1.0)[:, None]).astype(jnp.bfloat16)
    returned = lax.all_to_all(
        hidden.reshape(tensor_size, row_count, column_count),
        "tensor",
        split_axis=0,
        concat_axis=0,
        tiled=True,
    )
    hidden_f = (
        jnp.transpose(returned, (1, 0, 2)).astype(jnp.float32).reshape(row_count, head_count, head_dim)
    )
    mean_val = jnp.mean(hidden_f, axis=2, keepdims=True)
    centered = hidden_f - mean_val
    variance = jnp.mean(centered * centered, axis=2, keepdims=True)
    normed = (centered * lax.rsqrt(variance + 1e-05)).reshape(row_count, inner)
    return (normed * norm_gain * jax.nn.silu(output_gate.astype(jnp.float32))).astype(jnp.bfloat16)


def solution(mesh):
    in_specs = (
        P(("seq", "tensor"), None),
        P(("seq", "tensor"), None),
        P(("seq", "tensor"), None),
        P(("seq", "tensor"), None),
        P(("seq", "tensor"), None),
        P("seq"),
        P(("seq", "tensor"), None),
        P(),
    )
    out_specs = P(("seq", "tensor"), None)
    return jax.shard_map(
        on_device, mesh=mesh, in_specs=in_specs, out_specs=out_specs, check_vma=False
    )
```

```python
import math

import jax
import jax.numpy as jnp
from jax import lax
from jax.sharding import PartitionSpec as P

BLOCK = 256


precise = lax.Precision.HIGHEST


def split_dot(wide, narrow, dims):
    high = lax.reduce_precision(wide, exponent_bits=8, mantissa_bits=7)
    low = wide - high
    def one(part):
        return lax.dot_general(
            part.astype(jnp.bfloat16), narrow.astype(jnp.bfloat16), dims,
            preferred_element_type=jnp.float32,
        )
    return one(high) + one(low)


def split_dot_left(narrow, wide, dims):
    high = lax.reduce_precision(wide, exponent_bits=8, mantissa_bits=7)
    low = wide - high
    def one(part):
        return lax.dot_general(
            narrow.astype(jnp.bfloat16), part.astype(jnp.bfloat16), dims,
            preferred_element_type=jnp.float32,
        )
    return one(high) + one(low)


def shifted(value, axis, steps):
    count = lax.axis_size(axis)
    initial, last = (max(0, -steps), min(count, count - steps))
    return lax.ppermute(value, axis, [(source, source + steps) for source in range(initial, last)])


def shifted_narrow(value, axis, steps):
    return shifted(value.astype(jnp.bfloat16), axis, steps).astype(jnp.float32)


def meta_row(head_dim, column_count):
    return head_dim + head_dim // column_count


def pack_summary(query_all, key_all, value_all, gate_in, log_forget, segment_ids, key_scale):
    head_dim = key_all.shape[1]
    column_count = value_all.shape[1]
    cumulative = jnp.cumsum(log_forget)
    total_log = cumulative[-1]
    first_seg = segment_ids[0]
    last_seg = segment_ids[-1]
    tail_weight = jnp.exp(total_log - cumulative + gate_in) * (segment_ids == last_seg).astype(
        jnp.float32
    )
    scaled_keys = key_all.astype(jnp.float32) * (key_scale * tail_weight)[:, None]
    state = split_dot(scaled_keys, value_all, (((0,), (0,)), ((), ())))
    norm = jnp.sum(scaled_keys, axis=0)
    decay = jnp.exp(total_log) * (last_seg == first_seg).astype(jnp.float32)
    norm_rows = head_dim // column_count
    rows = meta_row(head_dim, column_count) + 1
    padded = -(-rows // 8) * 8
    lane = jnp.arange(column_count)
    decay_high = lax.reduce_precision(decay, exponent_bits=8, mantissa_bits=7)
    meta = jnp.where(
        lane == 0,
        decay_high,
        jnp.where(
            lane == 1,
            (first_seg + 1).astype(jnp.float32),
            jnp.where(
                lane == 2,
                (last_seg + 1).astype(jnp.float32),
                jnp.where(lane == 3, decay - decay_high, 0.0),
            ),
        ),
    )
    filler = jnp.zeros((padded - rows, column_count), jnp.float32)
    return jnp.concatenate(
        [state, norm.reshape(norm_rows, column_count), meta[None, :], filler], axis=0
    )


def combine_packed(earlier, later, head_dim):
    column_count = earlier.shape[1]
    row = meta_row(head_dim, column_count)
    e_decay, e_first, e_last = earlier[row, 0], earlier[row, 1], earlier[row, 2]
    l_decay, l_first, l_last = later[row, 0], later[row, 1], later[row, 2]
    linked = jnp.where((e_last == l_first) | (e_last <= 0.0) | (l_first <= 0.0), 1.0, 0.0)
    factor = jnp.where(l_first <= 0.0, 1.0, l_decay * linked)
    decay_part = jnp.where(e_first <= 0.0, l_decay, e_decay * factor)
    first_seg = jnp.where(e_first <= 0.0, l_first, e_first)
    last_seg = jnp.where(l_last <= 0.0, e_last, l_last)
    body = factor * earlier + later
    lane = jnp.arange(column_count)[None, :]
    rows = jnp.arange(earlier.shape[0])[:, None]
    meta = jnp.where(lane == 0, decay_part, jnp.where(lane == 1, first_seg, last_seg))
    return jnp.where((rows == row) & (lane < 3), meta, body)


def prefix_from_all(packed, head_dim):
    seq_count = lax.axis_size("seq")
    column_count = packed.shape[1]
    row = meta_row(head_dim, column_count)
    gathered = lax.all_gather(packed.astype(jnp.bfloat16), "seq")
    meta = gathered[:, row, :8].astype(jnp.float32)
    decay, first, last = meta[:, 0] + meta[:, 3], meta[:, 1], meta[:, 2]
    me = lax.axis_index("seq")
    order = jnp.arange(seq_count)
    previous_last = jnp.concatenate([jnp.zeros((1,), jnp.float32), last[:-1]])
    carry = decay * (previous_last == first).astype(jnp.float32)
    carry = jnp.where(order < me, carry, 1.0)
    after = jnp.cumprod(carry[::-1])[::-1]
    weight = jnp.concatenate([after[1:], jnp.ones((1,), jnp.float32)])
    weight = jnp.where(order < me, weight, 0.0)
    total = jnp.einsum("s,src->rc", weight, gathered.astype(jnp.float32))
    in_last = jnp.where(me > 0, last[jnp.maximum(me - 1, 0)], 0.0)
    lane = jnp.arange(column_count)[None, :]
    rows = jnp.arange(packed.shape[0])[:, None]
    return jnp.where((rows == row) & (lane == 2), in_last, total)


def on_device(
    queries, key_rows, values, input_gate, forget_gate, segment_ids, output_gate, norm_gain
):
    tensor_size = lax.axis_size("tensor")
    row_count, inner = queries.shape
    head_count = input_gate.shape[1]
    head_dim = inner // head_count
    group_size = tensor_size // head_count
    column_count = head_dim // group_size

    def spread_heads(array, width):
        shaped = array.reshape(row_count, head_count, 1, width)
        return jnp.broadcast_to(shaped, (row_count, head_count, group_size, width)).reshape(
            row_count, tensor_size, width
        )

    pair_q_k = jnp.stack(
        [
            queries.reshape(row_count, head_count, head_dim),
            key_rows.reshape(row_count, head_count, head_dim),
        ],
        axis=1,
    )
    pair_send = jnp.broadcast_to(
        jnp.transpose(pair_q_k, (2, 1, 0, 3))[:, None],
        (head_count, group_size // 2, 2, row_count, head_dim),
    ).reshape(tensor_size, row_count, head_dim)
    value_send = jnp.transpose(values.reshape(row_count, tensor_size, column_count), (1, 0, 2))
    body_width = row_count * (head_dim + column_count)
    gate_pair = jnp.stack([input_gate, forget_gate], axis=0)
    gate_send = jnp.broadcast_to(
        jnp.transpose(gate_pair, (2, 0, 1))[:, None], (head_count, group_size, 2, row_count)
    ).reshape(tensor_size, 2 * row_count)
    both_send = jnp.concatenate(
        [
            jnp.concatenate([pair_send, value_send], axis=2).reshape(tensor_size, body_width),
            gate_send,
        ],
        axis=1,
    )
    both_all = lax.all_to_all(both_send, "tensor", split_axis=0, concat_axis=0, tiled=True)
    gate_all = jnp.transpose(
        both_all[:, body_width:].reshape(tensor_size, 2, row_count), (1, 0, 2)
    ).reshape(2, tensor_size * row_count)
    both_all = both_all[:, :body_width].reshape(tensor_size * row_count, head_dim + column_count)
    own_part = both_all[:, :head_dim]
    value_all = both_all[:, head_dim:]
    other_part = lax.ppermute(
        own_part, "tensor", [(index, index ^ 1) for index in range(tensor_size)]
    )
    is_even = lax.axis_index("tensor") % 2 == 0
    query_all = jnp.where(is_even, own_part, other_part)
    key_all = jnp.where(is_even, other_part, own_part)
    token_count = query_all.shape[0]
    gate_f = gate_all.astype(jnp.float32)
    gate_in = gate_f[0]
    log_forget = jax.nn.log_sigmoid(gate_f[1])
    block_count = token_count // BLOCK
    key_scale = 1.0 / math.sqrt(head_dim)
    first_seg = segment_ids[0]

    packed = pack_summary(
        query_all, key_all, value_all, gate_in, log_forget, segment_ids, key_scale
    )
    incoming = prefix_from_all(packed, head_dim)
    in_row = meta_row(head_dim, column_count)
    in_state = incoming[:head_dim]
    in_norm = incoming[head_dim:in_row].reshape(head_dim)
    in_last = incoming[in_row, 2]

    row_ids = jnp.arange(BLOCK, dtype=jnp.int32)
    causal = row_ids[:, None] >= row_ids[None, :]

    def span_step(carry, block_in):
        cell_state, norm_vec, prev_seg, total_log = carry
        query_b, key_b, value_b, gate_b, forget_b, seg_b = block_in
        cumulative = jnp.cumsum(forget_b)
        allowed = causal & (seg_b[:, None] == seg_b[None, :])
        exponent = cumulative[:, None] - cumulative[None, :] + gate_b[None, :]
        weights = jnp.where(allowed, jnp.exp(jnp.where(allowed, exponent, 0.0)), 0.0)
        scores = (
            jnp.einsum("id,jd->ij", query_b, key_b, preferred_element_type=jnp.float32) * key_scale
        )
        weighted = weights * scores
        query_float = query_b.astype(jnp.float32)
        key_f = key_b.astype(jnp.float32) * key_scale
        value_f = value_b.astype(jnp.float32)
        numerator = split_dot(weighted, value_b, (((1,), (0,)), ((), ())))
        carried = jnp.exp(cumulative) * (seg_b == prev_seg).astype(jnp.float32)
        numerator = numerator + carried[:, None] * split_dot_left(
            query_b, cell_state, (((1,), (0,)), ((), ()))
        )
        q_norm = jnp.sum(weighted, axis=1) + carried * split_dot_left(
            query_b, norm_vec[:, None], (((1,), (0,)), ((), ()))
        )[:, 0]
        entry_factor = jnp.exp(total_log + cumulative) * (seg_b == first_seg).astype(jnp.float32)
        last_seg = seg_b[BLOCK - 1]
        tail_weight = jnp.exp(cumulative[BLOCK - 1] - cumulative + gate_b) * (
            seg_b == last_seg
        ).astype(jnp.float32)
        keep_factor = jnp.exp(cumulative[BLOCK - 1]) * (last_seg == prev_seg).astype(jnp.float32)
        scaled_keys = key_f * tail_weight[:, None]
        cell_state = keep_factor * cell_state + split_dot(
            scaled_keys, value_b, (((0,), (0,)), ((), ()))
        )
        norm_vec = keep_factor * norm_vec + jnp.sum(scaled_keys, axis=0)
        return (
            (cell_state, norm_vec, last_seg, total_log + cumulative[BLOCK - 1]),
            (numerator, q_norm, entry_factor),
        )

    initial = (
        jnp.zeros((head_dim, column_count), jnp.float32),
        jnp.zeros((head_dim,), jnp.float32),
        first_seg,
        jnp.zeros((), jnp.float32),
    )
    blocks_in = (
        query_all.reshape(block_count, BLOCK, head_dim),
        key_all.reshape(block_count, BLOCK, head_dim),
        value_all.reshape(block_count, BLOCK, column_count),
        gate_in.reshape(block_count, BLOCK),
        log_forget.reshape(block_count, BLOCK),
        segment_ids.reshape(block_count, BLOCK),
    )
    unused, outputs = lax.scan(span_step, initial, blocks_in)
    numerator = outputs[0].reshape(token_count, column_count)
    q_norm = outputs[1].reshape(token_count)
    entry_factor = outputs[2].reshape(token_count)

    linked = (in_last == (first_seg + 1).astype(jnp.float32)).astype(jnp.float32)
    scale_rows = entry_factor * linked
    numerator = numerator + scale_rows[:, None] * split_dot_left(
        query_all, in_state, (((1,), (0,)), ((), ()))
    )
    q_norm = q_norm + scale_rows * split_dot_left(
        query_all, in_norm[:, None], (((1,), (0,)), ((), ()))
    )[:, 0]
    hidden = (numerator / jnp.maximum(jnp.abs(q_norm), 1.0)[:, None]).astype(jnp.bfloat16)
    returned = lax.all_to_all(
        hidden.reshape(tensor_size, row_count, column_count),
        "tensor",
        split_axis=0,
        concat_axis=0,
        tiled=True,
    )
    hidden_f = (
        jnp.transpose(returned, (1, 0, 2)).astype(jnp.float32).reshape(row_count, head_count, head_dim)
    )
    mean_val = jnp.mean(hidden_f, axis=2, keepdims=True)
    centered = hidden_f - mean_val
    variance = jnp.mean(centered * centered, axis=2, keepdims=True)
    normed = (centered * lax.rsqrt(variance + 1e-05)).reshape(row_count, inner)
    return (normed * norm_gain * jax.nn.silu(output_gate.astype(jnp.float32))).astype(jnp.bfloat16)


def solution(mesh):
    in_specs = (
        P(("seq", "tensor"), None),
        P(("seq", "tensor"), None),
        P(("seq", "tensor"), None),
        P(("seq", "tensor"), None),
        P(("seq", "tensor"), None),
        P("seq"),
        P(("seq", "tensor"), None),
        P(),
    )
    out_specs = P(("seq", "tensor"), None)
    return jax.shard_map(
        on_device, mesh=mesh, in_specs=in_specs, out_specs=out_specs, check_vma=False
    )
```

```python
import math

import jax
import jax.numpy as jnp
import numpy as np
from jax import lax
from jax.sharding import Mesh
from jax.sharding import PartitionSpec as P


def split_dot(wide, narrow, dims):
    high = lax.reduce_precision(wide, exponent_bits=8, mantissa_bits=7)
    low = wide - high

    def one(part):
        return lax.dot_general(
            part.astype(jnp.bfloat16),
            narrow.astype(jnp.bfloat16),
            dims,
            preferred_element_type=jnp.float32,
        )

    return one(high) + one(low)


def split_dot_left(narrow, wide, dims):
    high = lax.reduce_precision(wide, exponent_bits=8, mantissa_bits=7)
    low = wide - high

    def one(part):
        return lax.dot_general(
            narrow.astype(jnp.bfloat16),
            part.astype(jnp.bfloat16),
            dims,
            preferred_element_type=jnp.float32,
        )

    return one(high) + one(low)


def meta_row(head_dim, column_count):
    return head_dim + head_dim // column_count


def with_meta(body, row, decay, first, last, low=None):
    lane = jnp.arange(body.shape[1])[None, :]
    rows = jnp.arange(body.shape[0])[:, None]
    values = jnp.where(lane == 0, decay, jnp.where(lane == 1, first, last))
    if low is not None:
        values = jnp.where(lane == 3, low, values)
    return jnp.where((rows == row) & (lane < (3 if low is None else 4)), values, body)


def pack_summary(key_all, value_all, gate_in, cumulative, segment_ids, key_scale):
    head_dim = key_all.shape[1]
    column_count = value_all.shape[1]
    total_log = cumulative[-1]
    first_seg = segment_ids[0]
    last_seg = segment_ids[-1]
    tail_weight = jnp.exp(total_log - cumulative + gate_in) * (segment_ids == last_seg).astype(
        jnp.float32
    )
    scaled_keys = key_all.astype(jnp.float32) * (key_scale * tail_weight)[:, None]
    state = split_dot(scaled_keys, value_all, (((0,), (0,)), ((), ())))
    norm = jnp.sum(scaled_keys, axis=0)
    decay = jnp.exp(total_log) * (last_seg == first_seg).astype(jnp.float32)
    norm_rows = head_dim // column_count
    rows = meta_row(head_dim, column_count) + 1
    padded = -(-rows // 8) * 8
    filler = jnp.zeros((padded - rows + 1, column_count), jnp.float32)
    body = jnp.concatenate([state, norm.reshape(norm_rows, column_count), filler], axis=0)
    decay_high = lax.reduce_precision(decay, exponent_bits=8, mantissa_bits=7)
    return with_meta(
        body,
        meta_row(head_dim, column_count),
        decay_high,
        (first_seg + 1).astype(jnp.float32),
        (last_seg + 1).astype(jnp.float32),
        decay - decay_high,
    )


def prefix_weights(decay, first, last, mine):
    count = decay.shape[0]
    order = jnp.arange(count)
    previous_last = jnp.concatenate([jnp.zeros((1,), jnp.float32), last[:-1]])
    carry = decay * (previous_last == first).astype(jnp.float32)
    carry = jnp.where((order < mine) & (order >= 1), carry, 1.0)
    after = jnp.cumprod(carry[::-1])[::-1]
    weight = jnp.concatenate([after[1:], jnp.ones((1,), jnp.float32)])
    weight = jnp.where(order < mine, weight, 0.0)
    combined_decay = decay[0] * after[1] if count > 1 else decay[0]
    combined_last = jnp.where(mine > 0, last[jnp.maximum(mine - 1, 0)], 0.0)
    combined_first = jnp.where(mine > 0, first[0], 0.0)
    return weight, combined_decay, combined_first, combined_last


def prefix_2d(packed, head_dim, row_axis, col_axis):
    column_count = packed.shape[1]
    row = meta_row(head_dim, column_count)
    row_size = lax.axis_size(row_axis)
    me_y = lax.axis_index(row_axis)
    me_x = lax.axis_index(col_axis)

    along_row = lax.all_gather(packed.astype(jnp.bfloat16), row_axis).astype(jnp.float32)
    meta = along_row[:, row, :4]
    decay, first, last = meta[:, 0] + meta[:, 3], meta[:, 1], meta[:, 2]
    w_row, decay_r, first_r, last_r = prefix_weights(decay, first, last, me_y)
    w_all, decay_t, first_t, last_t = prefix_weights(decay, first, last, row_size)
    row_part = jnp.einsum("s,src->rc", w_row, along_row)
    row_total = with_meta(
        jnp.einsum("s,src->rc", w_all, along_row), row, decay_t, first_t, last_t
    )

    along_col = lax.all_gather(row_total, col_axis)
    meta_c = along_col[:, row, :3]
    w_col, unused_decay, unused_first, last_p = prefix_weights(
        meta_c[:, 0], meta_c[:, 1], meta_c[:, 2], me_x
    )
    col_part = jnp.einsum("s,src->rc", w_col, along_col)

    has_row = me_y > 0
    factor = jnp.where(has_row, decay_r * (last_p == first_r).astype(jnp.float32), 1.0)
    state = factor * col_part + row_part
    in_last = jnp.where(has_row, last_r, last_p)
    return state, in_last


def on_device(
    queries, key_rows, values, input_gate, forget_gate, segment_ids, output_gate, norm_gain
):
    tensor_size = lax.axis_size("tensor")
    row_count, inner = queries.shape
    head_count = input_gate.shape[1]
    head_dim = inner // head_count
    group_size = tensor_size // head_count
    column_count = head_dim // group_size

    def spread_heads(array, width):
        shaped = array.reshape(row_count, head_count, 1, width)
        return jnp.broadcast_to(shaped, (row_count, head_count, group_size, width)).reshape(
            row_count, tensor_size, width
        )

    pair_q_k = jnp.stack(
        [
            queries.reshape(row_count, head_count, head_dim),
            key_rows.reshape(row_count, head_count, head_dim),
        ],
        axis=2,
    )
    pair_send = jnp.broadcast_to(
        pair_q_k[:, :, None], (row_count, head_count, group_size // 2, 2, head_dim)
    ).reshape(row_count, tensor_size, head_dim)
    value_send = values.reshape(row_count, tensor_size, column_count)
    both_send = jnp.concatenate([pair_send, value_send], axis=2)
    gate_send = spread_heads(jnp.stack([input_gate, forget_gate], axis=2), 2)
    both_all = lax.all_to_all(both_send, "tensor", split_axis=1, concat_axis=0, tiled=True)
    gate_all = lax.all_to_all(gate_send, "tensor", split_axis=1, concat_axis=0, tiled=True)
    both_all = both_all.reshape(-1, head_dim + column_count)
    own_part = both_all[:, :head_dim]
    value_all = both_all[:, head_dim:]
    other_part = lax.ppermute(
        own_part, "tensor", [(index, index ^ 1) for index in range(tensor_size)]
    )
    is_even = lax.axis_index("tensor") % 2 == 0
    query_all = jnp.where(is_even, own_part, other_part)
    key_all = jnp.where(is_even, other_part, own_part)
    token_count = query_all.shape[0]
    gate_f = gate_all.reshape(token_count, 2).astype(jnp.float32)
    gate_in = gate_f[:, 0]
    log_forget = jax.nn.log_sigmoid(gate_f[:, 1])
    key_scale = 1.0 / math.sqrt(head_dim)
    first_seg = segment_ids[0]
    cumulative = jnp.cumsum(log_forget)

    packed = pack_summary(key_all, value_all, gate_in, cumulative, segment_ids, key_scale)
    in_packed, in_last = prefix_2d(packed, head_dim, "sy", "sx")
    in_row = meta_row(head_dim, column_count)
    in_state = in_packed[:head_dim]
    in_norm = in_packed[head_dim:in_row].reshape(head_dim)

    token_ids = jnp.arange(token_count, dtype=jnp.int32)
    allowed = (token_ids[:, None] >= token_ids[None, :]) & (
        segment_ids[:, None] == segment_ids[None, :]
    )
    exponent = cumulative[:, None] - cumulative[None, :] + gate_in[None, :]
    weights = jnp.where(allowed, jnp.exp(jnp.where(allowed, exponent, 0.0)), 0.0)
    scores = (
        lax.dot_general(
            query_all, key_all, (((1,), (1,)), ((), ())), preferred_element_type=jnp.float32
        )
        * key_scale
    )
    weighted = weights * scores
    numerator = split_dot(weighted, value_all, (((1,), (0,)), ((), ())))
    q_norm = jnp.sum(weighted, axis=1)
    entry_factor = jnp.exp(cumulative) * (segment_ids == first_seg).astype(jnp.float32)

    linked = (in_last == (first_seg + 1).astype(jnp.float32)).astype(jnp.float32)
    scale_rows = entry_factor * linked
    numerator = numerator + scale_rows[:, None] * split_dot_left(
        query_all, in_state, (((1,), (0,)), ((), ()))
    )
    q_norm = q_norm + scale_rows * split_dot_left(
        query_all, in_norm[:, None], (((1,), (0,)), ((), ()))
    )[:, 0]
    hidden = (numerator / jnp.maximum(jnp.abs(q_norm), 1.0)[:, None]).astype(jnp.bfloat16)
    returned = lax.all_to_all(
        hidden.reshape(tensor_size, row_count, column_count),
        "tensor",
        split_axis=0,
        concat_axis=0,
        tiled=True,
    )
    hidden_f = (
        jnp.transpose(returned, (1, 0, 2)).astype(jnp.float32).reshape(row_count, head_count, head_dim)
    )
    mean_val = jnp.mean(hidden_f, axis=2, keepdims=True)
    centered = hidden_f - mean_val
    variance = jnp.mean(centered * centered, axis=2, keepdims=True)
    normed = (centered * lax.rsqrt(variance + 1e-05)).reshape(row_count, inner)
    return (normed * norm_gain * jax.nn.silu(output_gate.astype(jnp.float32))).astype(jnp.bfloat16)


def split_seq_mesh(mesh):
    devices = np.asarray(mesh.devices)
    seq_size, tensor_size = devices.shape
    row_size = len({int(d.coords[1]) for d in devices[:, 0]})
    return Mesh(
        devices.reshape(seq_size // row_size, row_size, tensor_size), ("sx", "sy", "tensor")
    )


def solution(mesh):
    split = split_seq_mesh(mesh)
    tokens = P(("sx", "sy", "tensor"), None)
    in_specs = (tokens, tokens, tokens, tokens, tokens, P(("sx", "sy")), tokens, P())
    return jax.shard_map(
        on_device, mesh=split, in_specs=in_specs, out_specs=tokens, check_vma=False
    )
```

```python
import math

import jax
import jax.numpy as jnp
import numpy as np
from jax import lax
from jax.sharding import Mesh
from jax.sharding import PartitionSpec as P


def split_dot(wide, narrow, dims):
    high = lax.reduce_precision(wide, exponent_bits=8, mantissa_bits=7)
    low = wide - high

    def one(part):
        return lax.dot_general(
            part.astype(jnp.bfloat16),
            narrow.astype(jnp.bfloat16),
            dims,
            preferred_element_type=jnp.float32,
        )

    return one(high) + one(low)


def split_dot_left(narrow, wide, dims):
    high = lax.reduce_precision(wide, exponent_bits=8, mantissa_bits=7)
    low = wide - high

    def one(part):
        return lax.dot_general(
            narrow.astype(jnp.bfloat16),
            part.astype(jnp.bfloat16),
            dims,
            preferred_element_type=jnp.float32,
        )

    return one(high) + one(low)


def meta_row(head_dim, column_count):
    return head_dim + head_dim // column_count


def with_meta(body, row, decay, first, last, low=None):
    lane = jnp.arange(body.shape[1])[None, :]
    rows = jnp.arange(body.shape[0])[:, None]
    values = jnp.where(lane == 0, decay, jnp.where(lane == 1, first, last))
    if low is not None:
        values = jnp.where(lane == 3, low, values)
    return jnp.where((rows == row) & (lane < (3 if low is None else 4)), values, body)


def pack_summary(key_all, value_all, gate_in, cumulative, segment_ids, key_scale):
    head_dim = key_all.shape[1]
    column_count = value_all.shape[1]
    total_log = cumulative[-1]
    first_seg = segment_ids[0]
    last_seg = segment_ids[-1]
    tail_weight = jnp.exp(total_log - cumulative + gate_in) * (segment_ids == last_seg).astype(
        jnp.float32
    )
    scaled_keys = key_all.astype(jnp.float32) * (key_scale * tail_weight)[:, None]
    state = split_dot(scaled_keys, value_all, (((0,), (0,)), ((), ())))
    norm = jnp.sum(scaled_keys, axis=0)
    decay = jnp.exp(total_log) * (last_seg == first_seg).astype(jnp.float32)
    norm_rows = head_dim // column_count
    rows = meta_row(head_dim, column_count) + 1
    padded = -(-rows // 8) * 8
    filler = jnp.zeros((padded - rows + 1, column_count), jnp.float32)
    body = jnp.concatenate([state, norm.reshape(norm_rows, column_count), filler], axis=0)
    decay_high = lax.reduce_precision(decay, exponent_bits=8, mantissa_bits=7)
    return with_meta(
        body,
        meta_row(head_dim, column_count),
        decay_high,
        (first_seg + 1).astype(jnp.float32),
        (last_seg + 1).astype(jnp.float32),
        decay - decay_high,
    )


def prefix_weights(decay, first, last, mine):
    count = decay.shape[0]
    order = jnp.arange(count)
    previous_last = jnp.concatenate([jnp.zeros((1,), jnp.float32), last[:-1]])
    carry = decay * (previous_last == first).astype(jnp.float32)
    carry = jnp.where((order < mine) & (order >= 1), carry, 1.0)
    after = jnp.cumprod(carry[::-1])[::-1]
    weight = jnp.concatenate([after[1:], jnp.ones((1,), jnp.float32)])
    weight = jnp.where(order < mine, weight, 0.0)
    combined_decay = decay[0] * after[1] if count > 1 else decay[0]
    combined_last = jnp.where(mine > 0, last[jnp.maximum(mine - 1, 0)], 0.0)
    combined_first = jnp.where(mine > 0, first[0], 0.0)
    return weight, combined_decay, combined_first, combined_last


def prefix_2d(packed, head_dim, row_axis, col_axis):
    column_count = packed.shape[1]
    row = meta_row(head_dim, column_count)
    row_size = lax.axis_size(row_axis)
    me_y = lax.axis_index(row_axis)
    me_x = lax.axis_index(col_axis)

    along_row = lax.all_gather(packed.astype(jnp.bfloat16), row_axis).astype(jnp.float32)
    meta = along_row[:, row, :4]
    decay, first, last = meta[:, 0] + meta[:, 3], meta[:, 1], meta[:, 2]
    w_row, decay_r, first_r, last_r = prefix_weights(decay, first, last, me_y)
    w_all, decay_t, first_t, last_t = prefix_weights(decay, first, last, row_size)
    row_part = jnp.einsum("s,src->rc", w_row, along_row)
    row_total = with_meta(
        jnp.einsum("s,src->rc", w_all, along_row), row, decay_t, first_t, last_t
    )

    along_col = lax.all_gather(row_total, col_axis)
    meta_c = along_col[:, row, :3]
    w_col, unused_decay, unused_first, last_p = prefix_weights(
        meta_c[:, 0], meta_c[:, 1], meta_c[:, 2], me_x
    )
    col_part = jnp.einsum("s,src->rc", w_col, along_col)

    has_row = me_y > 0
    factor = jnp.where(has_row, decay_r * (last_p == first_r).astype(jnp.float32), 1.0)
    state = factor * col_part + row_part
    in_last = jnp.where(has_row, last_r, last_p)
    return state, in_last


def prefix_from_all(packed, head_dim, row_axis, col_axis):
    column_count = packed.shape[1]
    row = meta_row(head_dim, column_count)
    axes = (col_axis, row_axis)
    gathered = lax.all_gather(packed.astype(jnp.bfloat16), axes)
    meta = gathered[:, row, :4].astype(jnp.float32)
    decay, first, last = meta[:, 0] + meta[:, 3], meta[:, 1], meta[:, 2]
    me = lax.axis_index(col_axis) * lax.axis_size(row_axis) + lax.axis_index(row_axis)
    weight, unused_decay, unused_first, in_last = prefix_weights(decay, first, last, me)
    state = jnp.einsum("s,src->rc", weight, gathered.astype(jnp.float32))
    return state, in_last


def on_device(
    queries, key_rows, values, input_gate, forget_gate, segment_ids, output_gate, norm_gain
):
    tensor_size = lax.axis_size("tensor")
    row_count, inner = queries.shape
    head_count = input_gate.shape[1]
    head_dim = inner // head_count
    group_size = tensor_size // head_count
    column_count = head_dim // group_size

    def spread_heads(array, width):
        shaped = array.reshape(row_count, head_count, 1, width)
        return jnp.broadcast_to(shaped, (row_count, head_count, group_size, width)).reshape(
            row_count, tensor_size, width
        )

    pair_q_k = jnp.stack(
        [
            queries.reshape(row_count, head_count, head_dim),
            key_rows.reshape(row_count, head_count, head_dim),
        ],
        axis=2,
    )
    pair_send = jnp.broadcast_to(
        pair_q_k[:, :, None], (row_count, head_count, group_size // 2, 2, head_dim)
    ).reshape(row_count, tensor_size, head_dim)
    value_send = values.reshape(row_count, tensor_size, column_count)
    both_send = jnp.concatenate([pair_send, value_send], axis=2)
    gate_send = spread_heads(jnp.stack([input_gate, forget_gate], axis=2), 2)
    both_all = lax.all_to_all(both_send, "tensor", split_axis=1, concat_axis=0, tiled=True)
    gate_all = lax.all_to_all(gate_send, "tensor", split_axis=1, concat_axis=0, tiled=True)
    both_all = both_all.reshape(-1, head_dim + column_count)
    own_part = both_all[:, :head_dim]
    value_all = both_all[:, head_dim:]
    other_part = lax.ppermute(
        own_part, "tensor", [(index, index ^ 1) for index in range(tensor_size)]
    )
    is_even = lax.axis_index("tensor") % 2 == 0
    query_all = jnp.where(is_even, own_part, other_part)
    key_all = jnp.where(is_even, other_part, own_part)
    token_count = query_all.shape[0]
    gate_f = gate_all.reshape(token_count, 2).astype(jnp.float32)
    gate_in = gate_f[:, 0]
    log_forget = jax.nn.log_sigmoid(gate_f[:, 1])
    key_scale = 1.0 / math.sqrt(head_dim)
    first_seg = segment_ids[0]
    cumulative = jnp.cumsum(log_forget)

    packed = pack_summary(key_all, value_all, gate_in, cumulative, segment_ids, key_scale)
    in_packed, in_last = prefix_from_all(packed, head_dim, "sy", "sx")
    in_row = meta_row(head_dim, column_count)
    in_state = in_packed[:head_dim]
    in_norm = in_packed[head_dim:in_row].reshape(head_dim)

    token_ids = jnp.arange(token_count, dtype=jnp.int32)
    allowed = (token_ids[:, None] >= token_ids[None, :]) & (
        segment_ids[:, None] == segment_ids[None, :]
    )
    exponent = cumulative[:, None] - cumulative[None, :] + gate_in[None, :]
    weights = jnp.where(allowed, jnp.exp(jnp.where(allowed, exponent, 0.0)), 0.0)
    scores = (
        lax.dot_general(
            query_all, key_all, (((1,), (1,)), ((), ())), preferred_element_type=jnp.float32
        )
        * key_scale
    )
    weighted = weights * scores
    numerator = split_dot(weighted, value_all, (((1,), (0,)), ((), ())))
    q_norm = jnp.sum(weighted, axis=1)
    entry_factor = jnp.exp(cumulative) * (segment_ids == first_seg).astype(jnp.float32)

    linked = (in_last == (first_seg + 1).astype(jnp.float32)).astype(jnp.float32)
    scale_rows = entry_factor * linked
    numerator = numerator + scale_rows[:, None] * split_dot_left(
        query_all, in_state, (((1,), (0,)), ((), ()))
    )
    q_norm = q_norm + scale_rows * split_dot_left(
        query_all, in_norm[:, None], (((1,), (0,)), ((), ()))
    )[:, 0]
    hidden = (numerator / jnp.maximum(jnp.abs(q_norm), 1.0)[:, None]).astype(jnp.bfloat16)
    returned = lax.all_to_all(
        hidden.reshape(tensor_size, row_count, column_count),
        "tensor",
        split_axis=0,
        concat_axis=0,
        tiled=True,
    )
    hidden_f = (
        jnp.transpose(returned, (1, 0, 2)).astype(jnp.float32).reshape(row_count, head_count, head_dim)
    )
    mean_val = jnp.mean(hidden_f, axis=2, keepdims=True)
    centered = hidden_f - mean_val
    variance = jnp.mean(centered * centered, axis=2, keepdims=True)
    normed = (centered * lax.rsqrt(variance + 1e-05)).reshape(row_count, inner)
    return (normed * norm_gain * jax.nn.silu(output_gate.astype(jnp.float32))).astype(jnp.bfloat16)


def split_seq_mesh(mesh):
    devices = np.asarray(mesh.devices)
    seq_size, tensor_size = devices.shape
    row_size = len({int(d.coords[1]) for d in devices[:, 0]})
    return Mesh(
        devices.reshape(seq_size // row_size, row_size, tensor_size), ("sx", "sy", "tensor")
    )


def solution(mesh):
    split = split_seq_mesh(mesh)
    tokens = P(("sx", "sy", "tensor"), None)
    in_specs = (tokens, tokens, tokens, tokens, tokens, P(("sx", "sy")), tokens, P())
    return jax.shard_map(
        on_device, mesh=split, in_specs=in_specs, out_specs=tokens, check_vma=False
    )
```

```python
import math

import jax
import jax.numpy as jnp
import numpy as np
from jax import lax
from jax.sharding import Mesh
from jax.sharding import PartitionSpec as P


def split_dot(wide, narrow, dims):
    high = lax.reduce_precision(wide, exponent_bits=8, mantissa_bits=7)
    low = wide - high

    def one(part):
        return lax.dot_general(
            part.astype(jnp.bfloat16),
            narrow.astype(jnp.bfloat16),
            dims,
            preferred_element_type=jnp.float32,
        )

    return one(high) + one(low)


def split_dot_left(narrow, wide, dims):
    high = lax.reduce_precision(wide, exponent_bits=8, mantissa_bits=7)
    low = wide - high

    def one(part):
        return lax.dot_general(
            narrow.astype(jnp.bfloat16),
            part.astype(jnp.bfloat16),
            dims,
            preferred_element_type=jnp.float32,
        )

    return one(high) + one(low)


def meta_row(head_dim, column_count):
    return head_dim + head_dim // column_count


def with_meta(body, row, decay, first, last, low=None):
    lane = jnp.arange(body.shape[1])[None, :]
    rows = jnp.arange(body.shape[0])[:, None]
    values = jnp.where(lane == 0, decay, jnp.where(lane == 1, first, last))
    if low is not None:
        values = jnp.where(lane == 3, low, values)
    return jnp.where((rows == row) & (lane < (3 if low is None else 4)), values, body)


def pack_summary(key_all, value_all, gate_in, cumulative, segment_ids, key_scale):
    head_dim = key_all.shape[1]
    column_count = value_all.shape[1]
    total_log = cumulative[-1]
    first_seg = segment_ids[0]
    last_seg = segment_ids[-1]
    tail_weight = jnp.exp(total_log - cumulative + gate_in) * (segment_ids == last_seg).astype(
        jnp.float32
    )
    scaled_keys = key_all.astype(jnp.float32) * (key_scale * tail_weight)[:, None]
    state = split_dot(scaled_keys, value_all, (((0,), (0,)), ((), ())))
    norm = jnp.sum(scaled_keys, axis=0)
    decay = jnp.exp(total_log) * (last_seg == first_seg).astype(jnp.float32)
    norm_rows = head_dim // column_count
    rows = meta_row(head_dim, column_count) + 1
    padded = -(-rows // 8) * 8
    filler = jnp.zeros((padded - rows + 1, column_count), jnp.float32)
    body = jnp.concatenate([state, norm.reshape(norm_rows, column_count), filler], axis=0)
    decay_high = lax.reduce_precision(decay, exponent_bits=8, mantissa_bits=7)
    return with_meta(
        body,
        meta_row(head_dim, column_count),
        decay_high,
        (first_seg + 1).astype(jnp.float32),
        (last_seg + 1).astype(jnp.float32),
        decay - decay_high,
    )


def prefix_weights(decay, first, last, mine):
    count = decay.shape[0]
    order = jnp.arange(count)
    previous_last = jnp.concatenate([jnp.zeros((1,), jnp.float32), last[:-1]])
    carry = decay * (previous_last == first).astype(jnp.float32)
    carry = jnp.where((order < mine) & (order >= 1), carry, 1.0)
    after = jnp.cumprod(carry[::-1])[::-1]
    weight = jnp.concatenate([after[1:], jnp.ones((1,), jnp.float32)])
    weight = jnp.where(order < mine, weight, 0.0)
    combined_decay = decay[0] * after[1] if count > 1 else decay[0]
    combined_last = jnp.where(mine > 0, last[jnp.maximum(mine - 1, 0)], 0.0)
    combined_first = jnp.where(mine > 0, first[0], 0.0)
    return weight, combined_decay, combined_first, combined_last


def prefix_2d(packed, head_dim, row_axis, col_axis):
    column_count = packed.shape[1]
    row = meta_row(head_dim, column_count)
    row_size = lax.axis_size(row_axis)
    me_y = lax.axis_index(row_axis)
    me_x = lax.axis_index(col_axis)

    along_row = lax.all_gather(packed.astype(jnp.bfloat16), row_axis).astype(jnp.float32)
    meta = along_row[:, row, :4]
    decay, first, last = meta[:, 0] + meta[:, 3], meta[:, 1], meta[:, 2]
    w_row, decay_r, first_r, last_r = prefix_weights(decay, first, last, me_y)
    w_all, decay_t, first_t, last_t = prefix_weights(decay, first, last, row_size)
    row_part = jnp.einsum("s,src->rc", w_row, along_row)
    row_total = with_meta(
        jnp.einsum("s,src->rc", w_all, along_row), row, decay_t, first_t, last_t
    )

    along_col = lax.all_gather(row_total, col_axis)
    meta_c = along_col[:, row, :3]
    w_col, unused_decay, unused_first, last_p = prefix_weights(
        meta_c[:, 0], meta_c[:, 1], meta_c[:, 2], me_x
    )
    col_part = jnp.einsum("s,src->rc", w_col, along_col)

    has_row = me_y > 0
    factor = jnp.where(has_row, decay_r * (last_p == first_r).astype(jnp.float32), 1.0)
    state = factor * col_part + row_part
    in_last = jnp.where(has_row, last_r, last_p)
    return state, in_last


def prefix_from_all(packed, head_dim, row_axis, col_axis):
    column_count = packed.shape[1]
    row = meta_row(head_dim, column_count)
    axes = (col_axis, row_axis)
    gathered = lax.all_gather(packed.astype(jnp.bfloat16), axes)
    meta = gathered[:, row, :4].astype(jnp.float32)
    decay, first, last = meta[:, 0] + meta[:, 3], meta[:, 1], meta[:, 2]
    me = lax.axis_index(col_axis) * lax.axis_size(row_axis) + lax.axis_index(row_axis)
    weight, unused_decay, unused_first, in_last = prefix_weights(decay, first, last, me)
    state = jnp.einsum("s,src->rc", weight, gathered.astype(jnp.float32))
    return state, in_last


def on_device(
    queries, key_rows, values, input_gate, forget_gate, segment_ids, output_gate, norm_gain
):
    tensor_size = lax.axis_size("tensor")
    row_count, inner = queries.shape
    head_count = input_gate.shape[1]
    head_dim = inner // head_count
    group_size = tensor_size // head_count
    column_count = head_dim // group_size

    def spread_heads(array, width):
        shaped = array.reshape(row_count, head_count, 1, width)
        return jnp.broadcast_to(shaped, (row_count, head_count, group_size, width)).reshape(
            row_count, tensor_size, width
        )

    half = head_dim // 2

    def halves_send(array):
        shaped = array.reshape(row_count, head_count, 1, 2, half)
        return jnp.broadcast_to(
            shaped, (row_count, head_count, group_size // 2, 2, half)
        ).reshape(row_count, tensor_size, half)

    is_even = lax.axis_index("tensor") % 2 == 0
    pairs = [(index, index ^ 1) for index in range(tensor_size)]

    def joined(own):
        other = lax.ppermute(own, "tensor", pairs)
        return jnp.where(
            is_even, jnp.concatenate([own, other], axis=1), jnp.concatenate([other, own], axis=1)
        )

    value_send = values.reshape(row_count, tensor_size, column_count)
    first_send = jnp.concatenate([halves_send(key_rows), value_send], axis=2)
    first_all = lax.all_to_all(first_send, "tensor", split_axis=1, concat_axis=0, tiled=True)
    first_all = first_all.reshape(-1, half + column_count)
    value_all = first_all[:, half:]
    key_all = joined(first_all[:, :half])
    gate_send = spread_heads(jnp.stack([input_gate, forget_gate], axis=2), 2)
    gate_all = lax.all_to_all(gate_send, "tensor", split_axis=1, concat_axis=0, tiled=True)
    query_half = lax.all_to_all(
        halves_send(queries), "tensor", split_axis=1, concat_axis=0, tiled=True
    ).reshape(-1, half)
    query_all = joined(query_half)
    token_count = query_all.shape[0]
    gate_f = gate_all.reshape(token_count, 2).astype(jnp.float32)
    gate_in = gate_f[:, 0]
    log_forget = jax.nn.log_sigmoid(gate_f[:, 1])
    key_scale = 1.0 / math.sqrt(head_dim)
    first_seg = segment_ids[0]
    cumulative = jnp.cumsum(log_forget)

    packed = pack_summary(key_all, value_all, gate_in, cumulative, segment_ids, key_scale)
    in_packed, in_last = prefix_from_all(packed, head_dim, "sy", "sx")
    in_row = meta_row(head_dim, column_count)
    in_state = in_packed[:head_dim]
    in_norm = in_packed[head_dim:in_row].reshape(head_dim)

    token_ids = jnp.arange(token_count, dtype=jnp.int32)
    allowed = (token_ids[:, None] >= token_ids[None, :]) & (
        segment_ids[:, None] == segment_ids[None, :]
    )
    exponent = cumulative[:, None] - cumulative[None, :] + gate_in[None, :]
    weights = jnp.where(allowed, jnp.exp(jnp.where(allowed, exponent, 0.0)), 0.0)
    scores = (
        lax.dot_general(
            query_all, key_all, (((1,), (1,)), ((), ())), preferred_element_type=jnp.float32
        )
        * key_scale
    )
    weighted = weights * scores
    numerator = split_dot(weighted, value_all, (((1,), (0,)), ((), ())))
    q_norm = jnp.sum(weighted, axis=1)
    entry_factor = jnp.exp(cumulative) * (segment_ids == first_seg).astype(jnp.float32)

    linked = (in_last == (first_seg + 1).astype(jnp.float32)).astype(jnp.float32)
    scale_rows = entry_factor * linked
    numerator = numerator + scale_rows[:, None] * split_dot_left(
        query_all, in_state, (((1,), (0,)), ((), ()))
    )
    q_norm = q_norm + scale_rows * split_dot_left(
        query_all, in_norm[:, None], (((1,), (0,)), ((), ()))
    )[:, 0]
    hidden = (numerator / jnp.maximum(jnp.abs(q_norm), 1.0)[:, None]).astype(jnp.bfloat16)
    returned = lax.all_to_all(
        hidden.reshape(tensor_size, row_count, column_count),
        "tensor",
        split_axis=0,
        concat_axis=0,
        tiled=True,
    )
    hidden_f = (
        jnp.transpose(returned, (1, 0, 2)).astype(jnp.float32).reshape(row_count, head_count, head_dim)
    )
    mean_val = jnp.mean(hidden_f, axis=2, keepdims=True)
    centered = hidden_f - mean_val
    variance = jnp.mean(centered * centered, axis=2, keepdims=True)
    normed = (centered * lax.rsqrt(variance + 1e-05)).reshape(row_count, inner)
    return (normed * norm_gain * jax.nn.silu(output_gate.astype(jnp.float32))).astype(jnp.bfloat16)


def split_seq_mesh(mesh):
    devices = np.asarray(mesh.devices)
    seq_size, tensor_size = devices.shape
    row_size = len({int(d.coords[1]) for d in devices[:, 0]})
    return Mesh(
        devices.reshape(seq_size // row_size, row_size, tensor_size), ("sx", "sy", "tensor")
    )


def solution(mesh):
    split = split_seq_mesh(mesh)
    tokens = P(("sx", "sy", "tensor"), None)
    in_specs = (tokens, tokens, tokens, tokens, tokens, P(("sx", "sy")), tokens, P())
    return jax.shard_map(
        on_device, mesh=split, in_specs=in_specs, out_specs=tokens, check_vma=False
    )
```

```python
import math

import jax
import jax.numpy as jnp
import numpy as np
from jax import lax
from jax.sharding import Mesh
from jax.sharding import PartitionSpec as P


def split_dot(wide, narrow, dims):
    high = lax.reduce_precision(wide, exponent_bits=8, mantissa_bits=7)
    low = wide - high

    def one(part):
        return lax.dot_general(
            part.astype(jnp.bfloat16),
            narrow.astype(jnp.bfloat16),
            dims,
            preferred_element_type=jnp.float32,
        )

    return one(high) + one(low)


def split_dot_left(narrow, wide, dims):
    high = lax.reduce_precision(wide, exponent_bits=8, mantissa_bits=7)
    low = wide - high

    def one(part):
        return lax.dot_general(
            narrow.astype(jnp.bfloat16),
            part.astype(jnp.bfloat16),
            dims,
            preferred_element_type=jnp.float32,
        )

    return one(high) + one(low)


def meta_row(head_dim, column_count):
    return head_dim + head_dim // column_count


def with_meta(body, row, decay, first, last, low=None):
    lane = jnp.arange(body.shape[1])[None, :]
    rows = jnp.arange(body.shape[0])[:, None]
    values = jnp.where(lane == 0, decay, jnp.where(lane == 1, first, last))
    if low is not None:
        values = jnp.where(lane == 3, low, values)
    return jnp.where((rows == row) & (lane < (3 if low is None else 4)), values, body)


def pack_summary(key_all, value_all, gate_in, cumulative, segment_ids, key_scale):
    head_dim = key_all.shape[1]
    column_count = value_all.shape[1]
    total_log = cumulative[-1]
    first_seg = segment_ids[0]
    last_seg = segment_ids[-1]
    tail_weight = jnp.exp(total_log - cumulative + gate_in) * (segment_ids == last_seg).astype(
        jnp.float32
    )
    token_weight = key_scale * tail_weight
    weighted_values = value_all.astype(jnp.float32) * token_weight[:, None]
    state = split_dot_left(key_all, weighted_values, (((0,), (0,)), ((), ())))
    norm = split_dot_left(key_all, token_weight[:, None], (((0,), (0,)), ((), ())))[:, 0]
    decay = jnp.exp(total_log) * (last_seg == first_seg).astype(jnp.float32)
    norm_rows = head_dim // column_count
    rows = meta_row(head_dim, column_count) + 1
    padded = -(-rows // 8) * 8
    filler = jnp.zeros((padded - rows + 1, column_count), jnp.float32)
    body = jnp.concatenate([state, norm.reshape(norm_rows, column_count), filler], axis=0)
    decay_high = lax.reduce_precision(decay, exponent_bits=8, mantissa_bits=7)
    return with_meta(
        body,
        meta_row(head_dim, column_count),
        decay_high,
        (first_seg + 1).astype(jnp.float32),
        (last_seg + 1).astype(jnp.float32),
        decay - decay_high,
    )


def prefix_weights(decay, first, last, mine):
    count = decay.shape[0]
    order = jnp.arange(count)
    previous_last = jnp.concatenate([jnp.zeros((1,), jnp.float32), last[:-1]])
    carry = decay * (previous_last == first).astype(jnp.float32)
    carry = jnp.where((order < mine) & (order >= 1), carry, 1.0)
    after = jnp.cumprod(carry[::-1])[::-1]
    weight = jnp.concatenate([after[1:], jnp.ones((1,), jnp.float32)])
    weight = jnp.where(order < mine, weight, 0.0)
    combined_decay = decay[0] * after[1] if count > 1 else decay[0]
    combined_last = jnp.where(mine > 0, last[jnp.maximum(mine - 1, 0)], 0.0)
    combined_first = jnp.where(mine > 0, first[0], 0.0)
    return weight, combined_decay, combined_first, combined_last


def prefix_2d(packed, head_dim, row_axis, col_axis):
    column_count = packed.shape[1]
    row = meta_row(head_dim, column_count)
    row_size = lax.axis_size(row_axis)
    me_y = lax.axis_index(row_axis)
    me_x = lax.axis_index(col_axis)

    along_row = lax.all_gather(packed.astype(jnp.bfloat16), row_axis).astype(jnp.float32)
    meta = along_row[:, row, :4]
    decay, first, last = meta[:, 0] + meta[:, 3], meta[:, 1], meta[:, 2]
    w_row, decay_r, first_r, last_r = prefix_weights(decay, first, last, me_y)
    w_all, decay_t, first_t, last_t = prefix_weights(decay, first, last, row_size)
    row_part = jnp.einsum("s,src->rc", w_row, along_row)
    row_total = with_meta(
        jnp.einsum("s,src->rc", w_all, along_row), row, decay_t, first_t, last_t
    )

    along_col = lax.all_gather(row_total, col_axis)
    meta_c = along_col[:, row, :3]
    w_col, unused_decay, unused_first, last_p = prefix_weights(
        meta_c[:, 0], meta_c[:, 1], meta_c[:, 2], me_x
    )
    col_part = jnp.einsum("s,src->rc", w_col, along_col)

    has_row = me_y > 0
    factor = jnp.where(has_row, decay_r * (last_p == first_r).astype(jnp.float32), 1.0)
    state = factor * col_part + row_part
    in_last = jnp.where(has_row, last_r, last_p)
    return state, in_last


def prefix_from_all(packed, head_dim, row_axis, col_axis):
    column_count = packed.shape[1]
    row = meta_row(head_dim, column_count)
    axes = (col_axis, row_axis)
    gathered = lax.all_gather(packed.astype(jnp.bfloat16), axes)
    meta = gathered[:, row, :4].astype(jnp.float32)
    decay, first, last = meta[:, 0] + meta[:, 3], meta[:, 1], meta[:, 2]
    me = lax.axis_index(col_axis) * lax.axis_size(row_axis) + lax.axis_index(row_axis)
    weight, unused_decay, unused_first, in_last = prefix_weights(decay, first, last, me)
    state = jnp.einsum("s,src->rc", weight, gathered.astype(jnp.float32))
    return state, in_last


def on_device(
    queries, key_rows, values, input_gate, forget_gate, segment_ids, output_gate, norm_gain
):
    tensor_size = lax.axis_size("tensor")
    row_count, inner = queries.shape
    head_count = input_gate.shape[1]
    head_dim = inner // head_count
    group_size = tensor_size // head_count
    column_count = head_dim // group_size

    def spread_heads(array, width):
        shaped = array.reshape(row_count, head_count, 1, width)
        return jnp.broadcast_to(shaped, (row_count, head_count, group_size, width)).reshape(
            row_count, tensor_size, width
        )

    half = head_dim // 2

    def halves_send(array):
        shaped = array.reshape(row_count, head_count, 1, 2, half)
        return jnp.broadcast_to(
            shaped, (row_count, head_count, group_size // 2, 2, half)
        ).reshape(row_count, tensor_size, half)

    is_even = lax.axis_index("tensor") % 2 == 0
    pairs = [(index, index ^ 1) for index in range(tensor_size)]

    def joined(own):
        other = lax.ppermute(own, "tensor", pairs)
        return jnp.where(
            is_even, jnp.concatenate([own, other], axis=1), jnp.concatenate([other, own], axis=1)
        )

    value_send = values.reshape(row_count, tensor_size, column_count)
    gate_lanes = 128
    gate_send = jnp.pad(
        spread_heads(jnp.stack([input_gate, forget_gate], axis=2), 2),
        ((0, 0), (0, 0), (0, gate_lanes - 2)),
    )
    first_send = jnp.concatenate([halves_send(key_rows), value_send, gate_send], axis=2)
    first_all = lax.all_to_all(first_send, "tensor", split_axis=1, concat_axis=0, tiled=True)
    first_all = first_all.reshape(-1, half + column_count + gate_lanes)
    value_all = first_all[:, half : half + column_count]
    gate_all = first_all[:, half + column_count : half + column_count + 2]
    key_all = joined(first_all[:, :half])
    query_half = lax.all_to_all(
        halves_send(queries), "tensor", split_axis=1, concat_axis=0, tiled=True
    ).reshape(-1, half)
    query_all = joined(query_half)
    token_count = query_all.shape[0]
    gate_f = gate_all.reshape(token_count, 2).astype(jnp.float32)
    gate_in = gate_f[:, 0]
    log_forget = jax.nn.log_sigmoid(gate_f[:, 1])
    key_scale = 1.0 / math.sqrt(head_dim)
    first_seg = segment_ids[0]
    cumulative = jnp.cumsum(log_forget)

    packed = pack_summary(key_all, value_all, gate_in, cumulative, segment_ids, key_scale)
    in_packed, in_last = prefix_from_all(packed, head_dim, "sy", "sx")
    in_row = meta_row(head_dim, column_count)
    in_state = in_packed[:head_dim]
    in_norm = in_packed[head_dim:in_row].reshape(head_dim)

    token_ids = jnp.arange(token_count, dtype=jnp.int32)
    allowed = (token_ids[:, None] >= token_ids[None, :]) & (
        segment_ids[:, None] == segment_ids[None, :]
    )
    exponent = cumulative[:, None] - cumulative[None, :] + gate_in[None, :]
    weights = jnp.where(allowed, jnp.exp(jnp.where(allowed, exponent, 0.0)), 0.0)
    scores = (
        lax.dot_general(
            query_all, key_all, (((1,), (1,)), ((), ())), preferred_element_type=jnp.float32
        )
        * key_scale
    )
    weighted = weights * scores
    numerator = split_dot(weighted, value_all, (((1,), (0,)), ((), ())))
    q_norm = jnp.sum(weighted, axis=1)
    entry_factor = jnp.exp(cumulative) * (segment_ids == first_seg).astype(jnp.float32)

    linked = (in_last == (first_seg + 1).astype(jnp.float32)).astype(jnp.float32)
    scale_rows = entry_factor * linked
    numerator = numerator + scale_rows[:, None] * split_dot_left(
        query_all, in_state, (((1,), (0,)), ((), ()))
    )
    q_norm = q_norm + scale_rows * split_dot_left(
        query_all, in_norm[:, None], (((1,), (0,)), ((), ()))
    )[:, 0]
    hidden = (numerator / jnp.maximum(jnp.abs(q_norm), 1.0)[:, None]).astype(jnp.bfloat16)
    returned = lax.all_to_all(
        hidden.reshape(tensor_size, row_count, column_count),
        "tensor",
        split_axis=0,
        concat_axis=0,
        tiled=True,
    )
    hidden_f = (
        jnp.transpose(returned, (1, 0, 2)).astype(jnp.float32).reshape(row_count, head_count, head_dim)
    )
    mean_val = jnp.mean(hidden_f, axis=2, keepdims=True)
    centered = hidden_f - mean_val
    variance = jnp.mean(centered * centered, axis=2, keepdims=True)
    normed = (centered * lax.rsqrt(variance + 1e-05)).reshape(row_count, inner)
    return (normed * norm_gain * jax.nn.silu(output_gate.astype(jnp.float32))).astype(jnp.bfloat16)


def split_seq_mesh(mesh):
    devices = np.asarray(mesh.devices)
    seq_size, tensor_size = devices.shape
    row_size = len({int(d.coords[1]) for d in devices[:, 0]})
    return Mesh(
        devices.reshape(seq_size // row_size, row_size, tensor_size), ("sx", "sy", "tensor")
    )


def solution(mesh):
    split = split_seq_mesh(mesh)
    tokens = P(("sx", "sy", "tensor"), None)
    in_specs = (tokens, tokens, tokens, tokens, tokens, P(("sx", "sy")), tokens, P())
    return jax.shard_map(
        on_device, mesh=split, in_specs=in_specs, out_specs=tokens, check_vma=False
    )
```

```python
import math

import jax
import jax.numpy as jnp
import numpy as np
from jax import lax
from jax.sharding import Mesh
from jax.sharding import PartitionSpec as P


def split_dot(wide, narrow, dims):
    high = lax.reduce_precision(wide, exponent_bits=8, mantissa_bits=7)
    low = wide - high

    def one(part):
        return lax.dot_general(
            part.astype(jnp.bfloat16),
            narrow.astype(jnp.bfloat16),
            dims,
            preferred_element_type=jnp.float32,
        )

    return one(high) + one(low)


def split_dot_left(narrow, wide, dims):
    high = lax.reduce_precision(wide, exponent_bits=8, mantissa_bits=7)
    low = wide - high

    def one(part):
        return lax.dot_general(
            narrow.astype(jnp.bfloat16),
            part.astype(jnp.bfloat16),
            dims,
            preferred_element_type=jnp.float32,
        )

    return one(high) + one(low)


def meta_row(head_dim, column_count):
    return head_dim + head_dim // column_count


def with_meta(body, row, decay, first, last, low=None):
    lane = jnp.arange(body.shape[1])[None, :]
    rows = jnp.arange(body.shape[0])[:, None]
    values = jnp.where(lane == 0, decay, jnp.where(lane == 1, first, last))
    if low is not None:
        values = jnp.where(lane == 3, low, values)
    return jnp.where((rows == row) & (lane < (3 if low is None else 4)), values, body)


def pack_summary(key_all, value_all, gate_in, cumulative, segment_ids, key_scale):
    head_dim = key_all.shape[1]
    column_count = value_all.shape[1]
    total_log = cumulative[-1]
    first_seg = segment_ids[0]
    last_seg = segment_ids[-1]
    tail_weight = jnp.exp(total_log - cumulative + gate_in) * (segment_ids == last_seg).astype(
        jnp.float32
    )
    token_weight = key_scale * tail_weight
    weighted_values = value_all.astype(jnp.float32) * token_weight[:, None]
    state = split_dot_left(key_all, weighted_values, (((0,), (0,)), ((), ())))
    norm = split_dot_left(key_all, token_weight[:, None], (((0,), (0,)), ((), ())))[:, 0]
    decay = jnp.exp(total_log) * (last_seg == first_seg).astype(jnp.float32)
    norm_rows = head_dim // column_count
    rows = meta_row(head_dim, column_count) + 1
    padded = -(-rows // 8) * 8
    filler = jnp.zeros((padded - rows + 1, column_count), jnp.float32)
    body = jnp.concatenate([state, norm.reshape(norm_rows, column_count), filler], axis=0)
    decay_high = lax.reduce_precision(decay, exponent_bits=8, mantissa_bits=7)
    return with_meta(
        body,
        meta_row(head_dim, column_count),
        decay_high,
        (first_seg + 1).astype(jnp.float32),
        (last_seg + 1).astype(jnp.float32),
        decay - decay_high,
    )


def prefix_weights(decay, first, last, mine):
    count = decay.shape[0]
    order = jnp.arange(count)
    previous_last = jnp.concatenate([jnp.zeros((1,), jnp.float32), last[:-1]])
    carry = decay * (previous_last == first).astype(jnp.float32)
    carry = jnp.where((order < mine) & (order >= 1), carry, 1.0)
    after = jnp.cumprod(carry[::-1])[::-1]
    weight = jnp.concatenate([after[1:], jnp.ones((1,), jnp.float32)])
    weight = jnp.where(order < mine, weight, 0.0)
    combined_decay = decay[0] * after[1] if count > 1 else decay[0]
    combined_last = jnp.where(mine > 0, last[jnp.maximum(mine - 1, 0)], 0.0)
    combined_first = jnp.where(mine > 0, first[0], 0.0)
    return weight, combined_decay, combined_first, combined_last


def prefix_2d(packed, head_dim, row_axis, col_axis):
    column_count = packed.shape[1]
    row = meta_row(head_dim, column_count)
    row_size = lax.axis_size(row_axis)
    me_y = lax.axis_index(row_axis)
    me_x = lax.axis_index(col_axis)

    along_row = lax.all_gather(packed.astype(jnp.bfloat16), row_axis).astype(jnp.float32)
    meta = along_row[:, row, :4]
    decay, first, last = meta[:, 0] + meta[:, 3], meta[:, 1], meta[:, 2]
    w_row, decay_r, first_r, last_r = prefix_weights(decay, first, last, me_y)
    w_all, decay_t, first_t, last_t = prefix_weights(decay, first, last, row_size)
    row_part = jnp.einsum("s,src->rc", w_row, along_row)
    row_total = with_meta(
        jnp.einsum("s,src->rc", w_all, along_row), row, decay_t, first_t, last_t
    )

    along_col = lax.all_gather(row_total, col_axis)
    meta_c = along_col[:, row, :3]
    w_col, unused_decay, unused_first, last_p = prefix_weights(
        meta_c[:, 0], meta_c[:, 1], meta_c[:, 2], me_x
    )
    col_part = jnp.einsum("s,src->rc", w_col, along_col)

    has_row = me_y > 0
    factor = jnp.where(has_row, decay_r * (last_p == first_r).astype(jnp.float32), 1.0)
    state = factor * col_part + row_part
    in_last = jnp.where(has_row, last_r, last_p)
    return state, in_last


def prefix_from_all(packed, head_dim, row_axis, col_axis):
    column_count = packed.shape[1]
    row = meta_row(head_dim, column_count)
    axes = (col_axis, row_axis)
    gathered = lax.all_gather(packed.astype(jnp.bfloat16), axes)
    meta = gathered[:, row, :4].astype(jnp.float32)
    decay, first, last = meta[:, 0] + meta[:, 3], meta[:, 1], meta[:, 2]
    me = lax.axis_index(col_axis) * lax.axis_size(row_axis) + lax.axis_index(row_axis)
    weight, unused_decay, unused_first, in_last = prefix_weights(decay, first, last, me)
    state = jnp.sum(gathered.astype(jnp.float32) * weight[:, None, None], axis=0)
    return state, in_last


def on_device(
    queries, key_rows, values, input_gate, forget_gate, segment_ids, output_gate, norm_gain
):
    tensor_size = lax.axis_size("tensor")
    row_count, inner = queries.shape
    head_count = input_gate.shape[1]
    head_dim = inner // head_count
    group_size = tensor_size // head_count
    column_count = head_dim // group_size

    def spread_heads(array, width):
        shaped = array.reshape(row_count, head_count, 1, width)
        return jnp.broadcast_to(shaped, (row_count, head_count, group_size, width)).reshape(
            row_count, tensor_size, width
        )

    half = head_dim // 2

    def halves_send(array):
        shaped = array.reshape(row_count, head_count, 1, 2, half)
        return jnp.broadcast_to(
            shaped, (row_count, head_count, group_size // 2, 2, half)
        ).reshape(row_count, tensor_size, half)

    is_even = lax.axis_index("tensor") % 2 == 0
    pairs = [(index, index ^ 1) for index in range(tensor_size)]

    def joined(own):
        other = lax.ppermute(own, "tensor", pairs)
        return jnp.where(
            is_even, jnp.concatenate([own, other], axis=1), jnp.concatenate([other, own], axis=1)
        )

    value_send = values.reshape(row_count, tensor_size, column_count)
    gate_lanes = 128
    gate_send = jnp.pad(
        spread_heads(jnp.stack([input_gate, forget_gate], axis=2), 2),
        ((0, 0), (0, 0), (0, gate_lanes - 2)),
    )
    first_send = jnp.concatenate([halves_send(key_rows), value_send, gate_send], axis=2)
    first_all = lax.all_to_all(first_send, "tensor", split_axis=1, concat_axis=0, tiled=True)
    first_all = first_all.reshape(-1, half + column_count + gate_lanes)
    value_all = first_all[:, half : half + column_count]
    gate_all = first_all[:, half + column_count : half + column_count + 2]
    key_all = joined(first_all[:, :half])
    query_half = lax.all_to_all(
        halves_send(queries), "tensor", split_axis=1, concat_axis=0, tiled=True
    ).reshape(-1, half)
    query_all = joined(query_half)
    token_count = query_all.shape[0]
    gate_f = gate_all.reshape(token_count, 2).astype(jnp.float32)
    gate_in = gate_f[:, 0]
    log_forget = jax.nn.log_sigmoid(gate_f[:, 1])
    key_scale = 1.0 / math.sqrt(head_dim)
    first_seg = segment_ids[0]
    cumulative = jnp.cumsum(log_forget)

    packed = pack_summary(key_all, value_all, gate_in, cumulative, segment_ids, key_scale)
    in_packed, in_last = prefix_from_all(packed, head_dim, "sy", "sx")
    in_row = meta_row(head_dim, column_count)
    in_state = in_packed[:head_dim]
    in_norm = in_packed[head_dim:in_row].reshape(head_dim)

    token_ids = jnp.arange(token_count, dtype=jnp.int32)
    allowed = (token_ids[:, None] >= token_ids[None, :]) & (
        segment_ids[:, None] == segment_ids[None, :]
    )
    exponent = cumulative[:, None] - cumulative[None, :] + gate_in[None, :]
    weights = jnp.where(allowed, jnp.exp(jnp.where(allowed, exponent, 0.0)), 0.0)
    scores = (
        lax.dot_general(
            query_all, key_all, (((1,), (1,)), ((), ())), preferred_element_type=jnp.float32
        )
        * key_scale
    )
    weighted = weights * scores
    numerator = split_dot(weighted, value_all, (((1,), (0,)), ((), ())))
    q_norm = jnp.sum(weighted, axis=1)
    entry_factor = jnp.exp(cumulative) * (segment_ids == first_seg).astype(jnp.float32)

    linked = (in_last == (first_seg + 1).astype(jnp.float32)).astype(jnp.float32)
    scale_rows = entry_factor * linked
    numerator = numerator + scale_rows[:, None] * split_dot_left(
        query_all, in_state, (((1,), (0,)), ((), ()))
    )
    q_norm = q_norm + scale_rows * split_dot_left(
        query_all, in_norm[:, None], (((1,), (0,)), ((), ()))
    )[:, 0]
    hidden = (numerator / jnp.maximum(jnp.abs(q_norm), 1.0)[:, None]).astype(jnp.bfloat16)
    returned = lax.all_to_all(
        hidden.reshape(tensor_size, row_count, column_count),
        "tensor",
        split_axis=0,
        concat_axis=0,
        tiled=True,
    )
    hidden_f = (
        jnp.transpose(returned, (1, 0, 2)).astype(jnp.float32).reshape(row_count, head_count, head_dim)
    )
    mean_val = jnp.mean(hidden_f, axis=2, keepdims=True)
    centered = hidden_f - mean_val
    variance = jnp.mean(centered * centered, axis=2, keepdims=True)
    normed = (centered * lax.rsqrt(variance + 1e-05)).reshape(row_count, inner)
    return (normed * norm_gain * jax.nn.silu(output_gate.astype(jnp.float32))).astype(jnp.bfloat16)


def split_seq_mesh(mesh):
    devices = np.asarray(mesh.devices)
    seq_size, tensor_size = devices.shape
    row_size = len({int(d.coords[1]) for d in devices[:, 0]})
    return Mesh(
        devices.reshape(seq_size // row_size, row_size, tensor_size), ("sx", "sy", "tensor")
    )


def solution(mesh):
    split = split_seq_mesh(mesh)
    tokens = P(("sx", "sy", "tensor"), None)
    in_specs = (tokens, tokens, tokens, tokens, tokens, P(("sx", "sy")), tokens, P())
    return jax.shard_map(
        on_device, mesh=split, in_specs=in_specs, out_specs=tokens, check_vma=False
    )
```

```python
import math

import jax
import jax.numpy as jnp
import numpy as np
from jax import lax
from jax.sharding import Mesh
from jax.sharding import PartitionSpec as P


def split_dot(wide, narrow, dims):
    high = lax.reduce_precision(wide, exponent_bits=8, mantissa_bits=7)
    low = wide - high

    def one(part):
        return lax.dot_general(
            part.astype(jnp.bfloat16),
            narrow.astype(jnp.bfloat16),
            dims,
            preferred_element_type=jnp.float32,
        )

    return one(high) + one(low)


def split_dot_left(narrow, wide, dims):
    high = lax.reduce_precision(wide, exponent_bits=8, mantissa_bits=7)
    low = wide - high

    def one(part):
        return lax.dot_general(
            narrow.astype(jnp.bfloat16),
            part.astype(jnp.bfloat16),
            dims,
            preferred_element_type=jnp.float32,
        )

    return one(high) + one(low)


def meta_row(head_dim, column_count):
    return head_dim + head_dim // column_count


def with_meta(body, row, decay, first, last, low=None):
    lane = jnp.arange(body.shape[1])[None, :]
    rows = jnp.arange(body.shape[0])[:, None]
    values = jnp.where(lane == 0, decay, jnp.where(lane == 1, first, last))
    if low is not None:
        values = jnp.where(lane == 3, low, values)
    return jnp.where((rows == row) & (lane < (3 if low is None else 4)), values, body)


def pack_summary(key_all, value_all, gate_in, cumulative, segment_ids, key_scale):
    head_dim = key_all.shape[1]
    column_count = value_all.shape[1]
    total_log = cumulative[-1]
    first_seg = segment_ids[0]
    last_seg = segment_ids[-1]
    tail_weight = jnp.exp(total_log - cumulative + gate_in) * (segment_ids == last_seg).astype(
        jnp.float32
    )
    token_weight = key_scale * tail_weight
    weighted_values = value_all.astype(jnp.float32) * token_weight[:, None]
    state = split_dot_left(key_all, weighted_values, (((0,), (0,)), ((), ())))
    norm = split_dot_left(key_all, token_weight[:, None], (((0,), (0,)), ((), ())))[:, 0]
    decay = jnp.exp(total_log) * (last_seg == first_seg).astype(jnp.float32)
    norm_rows = head_dim // column_count
    rows = meta_row(head_dim, column_count) + 1
    padded = -(-rows // 8) * 8
    filler = jnp.zeros((padded - rows + 1, column_count), jnp.float32)
    body = jnp.concatenate([state, norm.reshape(norm_rows, column_count), filler], axis=0)
    decay_high = lax.reduce_precision(decay, exponent_bits=8, mantissa_bits=7)
    return with_meta(
        body,
        meta_row(head_dim, column_count),
        decay_high,
        (first_seg + 1).astype(jnp.float32),
        (last_seg + 1).astype(jnp.float32),
        decay - decay_high,
    )


def prefix_weights(decay, first, last, mine):
    count = decay.shape[0]
    order = jnp.arange(count)
    previous_last = jnp.concatenate([jnp.zeros((1,), jnp.float32), last[:-1]])
    carry = decay * (previous_last == first).astype(jnp.float32)
    carry = jnp.where((order < mine) & (order >= 1), carry, 1.0)
    after = jnp.cumprod(carry[::-1])[::-1]
    weight = jnp.concatenate([after[1:], jnp.ones((1,), jnp.float32)])
    weight = jnp.where(order < mine, weight, 0.0)
    combined_decay = decay[0] * after[1] if count > 1 else decay[0]
    combined_last = jnp.where(mine > 0, last[jnp.maximum(mine - 1, 0)], 0.0)
    combined_first = jnp.where(mine > 0, first[0], 0.0)
    return weight, combined_decay, combined_first, combined_last


def prefix_2d(packed, head_dim, row_axis, col_axis):
    column_count = packed.shape[1]
    row = meta_row(head_dim, column_count)
    row_size = lax.axis_size(row_axis)
    me_y = lax.axis_index(row_axis)
    me_x = lax.axis_index(col_axis)

    along_row = lax.all_gather(packed.astype(jnp.bfloat16), row_axis).astype(jnp.float32)
    meta = along_row[:, row, :4]
    decay, first, last = meta[:, 0] + meta[:, 3], meta[:, 1], meta[:, 2]
    w_row, decay_r, first_r, last_r = prefix_weights(decay, first, last, me_y)
    w_all, decay_t, first_t, last_t = prefix_weights(decay, first, last, row_size)
    row_part = jnp.einsum("s,src->rc", w_row, along_row)
    row_total = with_meta(
        jnp.einsum("s,src->rc", w_all, along_row), row, decay_t, first_t, last_t
    )

    along_col = lax.all_gather(row_total, col_axis)
    meta_c = along_col[:, row, :3]
    w_col, unused_decay, unused_first, last_p = prefix_weights(
        meta_c[:, 0], meta_c[:, 1], meta_c[:, 2], me_x
    )
    col_part = jnp.einsum("s,src->rc", w_col, along_col)

    has_row = me_y > 0
    factor = jnp.where(has_row, decay_r * (last_p == first_r).astype(jnp.float32), 1.0)
    state = factor * col_part + row_part
    in_last = jnp.where(has_row, last_r, last_p)
    return state, in_last


def prefix_from_all(packed, head_dim, row_axis, col_axis):
    column_count = packed.shape[1]
    row = meta_row(head_dim, column_count)
    axes = (col_axis, row_axis)
    gathered = lax.all_gather(packed.astype(jnp.bfloat16), axes)
    meta = gathered[:, row, :4].astype(jnp.float32)
    decay, first, last = meta[:, 0] + meta[:, 3], meta[:, 1], meta[:, 2]
    me = lax.axis_index(col_axis) * lax.axis_size(row_axis) + lax.axis_index(row_axis)
    weight, unused_decay, unused_first, in_last = prefix_weights(decay, first, last, me)
    state = jnp.sum(gathered.astype(jnp.float32) * weight[:, None, None], axis=0)
    return state, in_last


def prefix_radix(packed, head_dim, row_axis, col_axis):
    column_count = packed.shape[1]
    row = meta_row(head_dim, column_count)
    axes = (col_axis, row_axis)
    count = lax.axis_size(col_axis) * lax.axis_size(row_axis)

    def moved(value, steps):
        pairs = [(source, source + steps) for source in range(count - steps)]
        return lax.ppermute(value, axes, pairs)

    def merged(parts):
        stack = jnp.stack(parts, axis=0)
        meta = stack[:, row, :4]
        decay, first, last = meta[:, 0] + meta[:, 3], meta[:, 1], meta[:, 2]
        weight, decay_c, unused_first, last_c = prefix_weights(decay, first, last, len(parts))
        real = first > 0.0
        first_real = jnp.max(jnp.where(real, first, 0.0) * (jnp.cumsum(real) == 1))
        body = jnp.sum(stack * weight[:, None, None], axis=0)
        return body, decay_c, first_real, last_c

    body, decay_1, first_1, last_1 = merged(
        [moved(packed, 3), moved(packed, 2), moved(packed, 1), packed]
    )
    span = with_meta(body, row, decay_1, first_1, last_1, jnp.zeros((), jnp.float32))
    state, unused_decay, unused_first, in_last = merged(
        [moved(span, 13), moved(span, 9), moved(span, 5), moved(span, 1)]
    )
    return state, in_last


def on_device(
    queries, key_rows, values, input_gate, forget_gate, segment_ids, output_gate, norm_gain
):
    tensor_size = lax.axis_size("tensor")
    row_count, inner = queries.shape
    head_count = input_gate.shape[1]
    head_dim = inner // head_count
    group_size = tensor_size // head_count
    column_count = head_dim // group_size

    def spread_heads(array, width):
        shaped = array.reshape(row_count, head_count, 1, width)
        return jnp.broadcast_to(shaped, (row_count, head_count, group_size, width)).reshape(
            row_count, tensor_size, width
        )

    half = head_dim // 2

    def halves_send(array):
        shaped = array.reshape(row_count, head_count, 1, 2, half)
        return jnp.broadcast_to(
            shaped, (row_count, head_count, group_size // 2, 2, half)
        ).reshape(row_count, tensor_size, half)

    is_even = lax.axis_index("tensor") % 2 == 0
    pairs = [(index, index ^ 1) for index in range(tensor_size)]

    def joined(own):
        other = lax.ppermute(own, "tensor", pairs)
        return jnp.where(
            is_even, jnp.concatenate([own, other], axis=1), jnp.concatenate([other, own], axis=1)
        )

    value_send = values.reshape(row_count, tensor_size, column_count)
    gate_lanes = 128
    gate_send = jnp.pad(
        spread_heads(jnp.stack([input_gate, forget_gate], axis=2), 2),
        ((0, 0), (0, 0), (0, gate_lanes - 2)),
    )
    first_send = jnp.concatenate([halves_send(key_rows), value_send, gate_send], axis=2)
    first_all = lax.all_to_all(first_send, "tensor", split_axis=1, concat_axis=0, tiled=True)
    first_all = first_all.reshape(-1, half + column_count + gate_lanes)
    value_all = first_all[:, half : half + column_count]
    gate_all = first_all[:, half + column_count : half + column_count + 2]
    key_all = joined(first_all[:, :half])
    query_half = lax.all_to_all(
        halves_send(queries), "tensor", split_axis=1, concat_axis=0, tiled=True
    ).reshape(-1, half)
    query_all = joined(query_half)
    token_count = query_all.shape[0]
    gate_f = gate_all.reshape(token_count, 2).astype(jnp.float32)
    gate_in = gate_f[:, 0]
    log_forget = jax.nn.log_sigmoid(gate_f[:, 1])
    key_scale = 1.0 / math.sqrt(head_dim)
    first_seg = segment_ids[0]
    cumulative = jnp.cumsum(log_forget)

    packed = pack_summary(key_all, value_all, gate_in, cumulative, segment_ids, key_scale)
    in_packed, in_last = prefix_radix(packed, head_dim, "sy", "sx")
    in_row = meta_row(head_dim, column_count)
    in_state = in_packed[:head_dim]
    in_norm = in_packed[head_dim:in_row].reshape(head_dim)

    token_ids = jnp.arange(token_count, dtype=jnp.int32)
    allowed = (token_ids[:, None] >= token_ids[None, :]) & (
        segment_ids[:, None] == segment_ids[None, :]
    )
    exponent = cumulative[:, None] - cumulative[None, :] + gate_in[None, :]
    weights = jnp.where(allowed, jnp.exp(jnp.where(allowed, exponent, 0.0)), 0.0)
    scores = (
        lax.dot_general(
            query_all, key_all, (((1,), (1,)), ((), ())), preferred_element_type=jnp.float32
        )
        * key_scale
    )
    weighted = weights * scores
    numerator = split_dot(weighted, value_all, (((1,), (0,)), ((), ())))
    q_norm = jnp.sum(weighted, axis=1)
    entry_factor = jnp.exp(cumulative) * (segment_ids == first_seg).astype(jnp.float32)

    linked = (in_last == (first_seg + 1).astype(jnp.float32)).astype(jnp.float32)
    scale_rows = entry_factor * linked
    numerator = numerator + scale_rows[:, None] * split_dot_left(
        query_all, in_state, (((1,), (0,)), ((), ()))
    )
    q_norm = q_norm + scale_rows * split_dot_left(
        query_all, in_norm[:, None], (((1,), (0,)), ((), ()))
    )[:, 0]
    hidden = (numerator / jnp.maximum(jnp.abs(q_norm), 1.0)[:, None]).astype(jnp.bfloat16)
    returned = lax.all_to_all(
        hidden.reshape(tensor_size, row_count, column_count),
        "tensor",
        split_axis=0,
        concat_axis=0,
        tiled=True,
    )
    hidden_f = (
        jnp.transpose(returned, (1, 0, 2)).astype(jnp.float32).reshape(row_count, head_count, head_dim)
    )
    mean_val = jnp.mean(hidden_f, axis=2, keepdims=True)
    centered = hidden_f - mean_val
    variance = jnp.mean(centered * centered, axis=2, keepdims=True)
    normed = (centered * lax.rsqrt(variance + 1e-05)).reshape(row_count, inner)
    return (normed * norm_gain * jax.nn.silu(output_gate.astype(jnp.float32))).astype(jnp.bfloat16)


def split_seq_mesh(mesh):
    devices = np.asarray(mesh.devices)
    seq_size, tensor_size = devices.shape
    row_size = len({int(d.coords[1]) for d in devices[:, 0]})
    return Mesh(
        devices.reshape(seq_size // row_size, row_size, tensor_size), ("sx", "sy", "tensor")
    )


def solution(mesh):
    split = split_seq_mesh(mesh)
    tokens = P(("sx", "sy", "tensor"), None)
    in_specs = (tokens, tokens, tokens, tokens, tokens, P(("sx", "sy")), tokens, P())
    return jax.shard_map(
        on_device, mesh=split, in_specs=in_specs, out_specs=tokens, check_vma=False
    )
```

```python
import math

import jax
import jax.numpy as jnp
import numpy as np
from jax import lax
from jax.sharding import Mesh
from jax.sharding import PartitionSpec as P


def split_dot(wide, narrow, dims):
    high = lax.reduce_precision(wide, exponent_bits=8, mantissa_bits=7)
    low = wide - high

    def one(part):
        return lax.dot_general(
            part.astype(jnp.bfloat16),
            narrow.astype(jnp.bfloat16),
            dims,
            preferred_element_type=jnp.float32,
        )

    return one(high) + one(low)


def split_dot_left(narrow, wide, dims):
    high = lax.reduce_precision(wide, exponent_bits=8, mantissa_bits=7)
    low = wide - high

    def one(part):
        return lax.dot_general(
            narrow.astype(jnp.bfloat16),
            part.astype(jnp.bfloat16),
            dims,
            preferred_element_type=jnp.float32,
        )

    return one(high) + one(low)


def meta_row(head_dim, column_count):
    return head_dim + head_dim // column_count


def with_meta(body, row, decay, first, last, low=None):
    lane = jnp.arange(body.shape[1])[None, :]
    rows = jnp.arange(body.shape[0])[:, None]
    values = jnp.where(lane == 0, decay, jnp.where(lane == 1, first, last))
    if low is not None:
        values = jnp.where(lane == 3, low, values)
    return jnp.where((rows == row) & (lane < (3 if low is None else 4)), values, body)


def pack_summary(key_own, key_other, is_even, value_all, gate_in, cumulative, segment_ids, key_scale):
    head_dim = key_own.shape[1] * 2
    column_count = value_all.shape[1]
    total_log = cumulative[-1]
    first_seg = segment_ids[0]
    last_seg = segment_ids[-1]
    tail_weight = jnp.exp(total_log - cumulative + gate_in) * (segment_ids == last_seg).astype(
        jnp.float32
    )
    token_weight = key_scale * tail_weight
    weighted_values = value_all.astype(jnp.float32) * token_weight[:, None]
    both = jnp.concatenate([weighted_values, token_weight[:, None]], axis=1)
    own_rows = split_dot_left(key_own, both, (((0,), (0,)), ((), ())))
    other_rows = split_dot_left(key_other, both, (((0,), (0,)), ((), ())))
    rows_all = jnp.where(
        is_even,
        jnp.concatenate([own_rows, other_rows], axis=0),
        jnp.concatenate([other_rows, own_rows], axis=0),
    )
    state = rows_all[:, :column_count]
    norm = rows_all[:, column_count]
    decay = jnp.exp(total_log) * (last_seg == first_seg).astype(jnp.float32)
    norm_rows = head_dim // column_count
    rows = meta_row(head_dim, column_count) + 1
    padded = -(-rows // 8) * 8
    filler = jnp.zeros((padded - rows + 1, column_count), jnp.float32)
    body = jnp.concatenate([state, norm.reshape(norm_rows, column_count), filler], axis=0)
    decay_high = lax.reduce_precision(decay, exponent_bits=8, mantissa_bits=7)
    return with_meta(
        body,
        meta_row(head_dim, column_count),
        decay_high,
        (first_seg + 1).astype(jnp.float32),
        (last_seg + 1).astype(jnp.float32),
        decay - decay_high,
    )


def prefix_weights(decay, first, last, mine):
    count = decay.shape[0]
    order = jnp.arange(count)
    previous_last = jnp.concatenate([jnp.zeros((1,), jnp.float32), last[:-1]])
    carry = decay * (previous_last == first).astype(jnp.float32)
    carry = jnp.where((order < mine) & (order >= 1), carry, 1.0)
    after = jnp.cumprod(carry[::-1])[::-1]
    weight = jnp.concatenate([after[1:], jnp.ones((1,), jnp.float32)])
    weight = jnp.where(order < mine, weight, 0.0)
    combined_decay = decay[0] * after[1] if count > 1 else decay[0]
    combined_last = jnp.where(mine > 0, last[jnp.maximum(mine - 1, 0)], 0.0)
    combined_first = jnp.where(mine > 0, first[0], 0.0)
    return weight, combined_decay, combined_first, combined_last


def prefix_2d(packed, head_dim, row_axis, col_axis):
    column_count = packed.shape[1]
    row = meta_row(head_dim, column_count)
    row_size = lax.axis_size(row_axis)
    me_y = lax.axis_index(row_axis)
    me_x = lax.axis_index(col_axis)

    along_row = lax.all_gather(packed.astype(jnp.bfloat16), row_axis).astype(jnp.float32)
    meta = along_row[:, row, :4]
    decay, first, last = meta[:, 0] + meta[:, 3], meta[:, 1], meta[:, 2]
    w_row, decay_r, first_r, last_r = prefix_weights(decay, first, last, me_y)
    w_all, decay_t, first_t, last_t = prefix_weights(decay, first, last, row_size)
    row_part = jnp.einsum("s,src->rc", w_row, along_row)
    row_total = with_meta(
        jnp.einsum("s,src->rc", w_all, along_row), row, decay_t, first_t, last_t
    )

    along_col = lax.all_gather(row_total, col_axis)
    meta_c = along_col[:, row, :3]
    w_col, unused_decay, unused_first, last_p = prefix_weights(
        meta_c[:, 0], meta_c[:, 1], meta_c[:, 2], me_x
    )
    col_part = jnp.einsum("s,src->rc", w_col, along_col)

    has_row = me_y > 0
    factor = jnp.where(has_row, decay_r * (last_p == first_r).astype(jnp.float32), 1.0)
    state = factor * col_part + row_part
    in_last = jnp.where(has_row, last_r, last_p)
    return state, in_last


def prefix_from_all(packed, head_dim, row_axis, col_axis):
    column_count = packed.shape[1]
    row = meta_row(head_dim, column_count)
    axes = (col_axis, row_axis)
    gathered = lax.all_gather(packed.astype(jnp.bfloat16), axes)
    meta = gathered[:, row, :4].astype(jnp.float32)
    decay, first, last = meta[:, 0] + meta[:, 3], meta[:, 1], meta[:, 2]
    me = lax.axis_index(col_axis) * lax.axis_size(row_axis) + lax.axis_index(row_axis)
    weight, unused_decay, unused_first, in_last = prefix_weights(decay, first, last, me)
    state = jnp.einsum("s,src->rc", weight, gathered.astype(jnp.float32))
    return state, in_last


def on_device(
    queries, key_rows, values, input_gate, forget_gate, segment_ids, output_gate, norm_gain
):
    tensor_size = lax.axis_size("tensor")
    row_count, inner = queries.shape
    head_count = input_gate.shape[1]
    head_dim = inner // head_count
    group_size = tensor_size // head_count
    column_count = head_dim // group_size

    def spread_heads(array, width):
        shaped = array.reshape(row_count, head_count, 1, width)
        return jnp.broadcast_to(shaped, (row_count, head_count, group_size, width)).reshape(
            row_count, tensor_size, width
        )

    half = head_dim // 2

    def halves_send(array):
        shaped = array.reshape(row_count, head_count, 1, 2, half)
        return jnp.broadcast_to(
            shaped, (row_count, head_count, group_size // 2, 2, half)
        ).reshape(row_count, tensor_size, half)

    is_even = lax.axis_index("tensor") % 2 == 0
    pairs = [(index, index ^ 1) for index in range(tensor_size)]

    def joined(own, other):
        return jnp.where(
            is_even, jnp.concatenate([own, other], axis=1), jnp.concatenate([other, own], axis=1)
        )

    value_send = values.reshape(row_count, tensor_size, column_count)
    gate_lanes = 128
    gate_send = jnp.pad(
        spread_heads(jnp.stack([input_gate, forget_gate], axis=2), 2),
        ((0, 0), (0, 0), (0, gate_lanes - 2)),
    )
    first_send = jnp.concatenate([halves_send(key_rows), value_send, gate_send], axis=2)
    first_all = lax.all_to_all(first_send, "tensor", split_axis=1, concat_axis=0, tiled=True)
    first_all = first_all.reshape(-1, half + column_count + gate_lanes)
    value_all = first_all[:, half : half + column_count]
    gate_all = first_all[:, half + column_count : half + column_count + 2]
    key_own = first_all[:, :half]
    key_other = lax.ppermute(key_own, "tensor", pairs)
    key_all = joined(key_own, key_other)
    query_half = lax.all_to_all(
        halves_send(queries), "tensor", split_axis=1, concat_axis=0, tiled=True
    ).reshape(-1, half)
    query_all = joined(query_half, lax.ppermute(query_half, "tensor", pairs))
    token_count = query_all.shape[0]
    gate_f = gate_all.reshape(token_count, 2).astype(jnp.float32)
    gate_in = gate_f[:, 0]
    log_forget = jax.nn.log_sigmoid(gate_f[:, 1])
    key_scale = 1.0 / math.sqrt(head_dim)
    first_seg = segment_ids[0]
    cumulative = jnp.cumsum(log_forget)

    packed = pack_summary(
        key_own, key_other, is_even, value_all, gate_in, cumulative, segment_ids, key_scale
    )
    in_packed, in_last = prefix_from_all(packed, head_dim, "sy", "sx")
    in_row = meta_row(head_dim, column_count)
    in_state = in_packed[:head_dim]
    in_norm = in_packed[head_dim:in_row].reshape(head_dim)

    token_ids = jnp.arange(token_count, dtype=jnp.int32)
    allowed = (token_ids[:, None] >= token_ids[None, :]) & (
        segment_ids[:, None] == segment_ids[None, :]
    )
    exponent = cumulative[:, None] - cumulative[None, :] + gate_in[None, :]
    weights = jnp.where(allowed, jnp.exp(jnp.where(allowed, exponent, 0.0)), 0.0)
    scores = (
        lax.dot_general(
            query_all, key_all, (((1,), (1,)), ((), ())), preferred_element_type=jnp.float32
        )
        * key_scale
    )
    weighted = weights * scores
    numerator = split_dot(weighted, value_all, (((1,), (0,)), ((), ())))
    q_norm = jnp.sum(weighted, axis=1)
    entry_factor = jnp.exp(cumulative) * (segment_ids == first_seg).astype(jnp.float32)

    linked = (in_last == (first_seg + 1).astype(jnp.float32)).astype(jnp.float32)
    scale_rows = entry_factor * linked
    numerator = numerator + scale_rows[:, None] * split_dot_left(
        query_all, in_state, (((1,), (0,)), ((), ()))
    )
    q_norm = q_norm + scale_rows * split_dot_left(
        query_all, in_norm[:, None], (((1,), (0,)), ((), ()))
    )[:, 0]
    hidden = (numerator / jnp.maximum(jnp.abs(q_norm), 1.0)[:, None]).astype(jnp.bfloat16)
    returned = lax.all_to_all(
        hidden.reshape(tensor_size, row_count, column_count),
        "tensor",
        split_axis=0,
        concat_axis=0,
        tiled=True,
    )
    hidden_f = (
        jnp.transpose(returned, (1, 0, 2)).astype(jnp.float32).reshape(row_count, head_count, head_dim)
    )
    mean_val = jnp.mean(hidden_f, axis=2, keepdims=True)
    centered = hidden_f - mean_val
    variance = jnp.mean(centered * centered, axis=2, keepdims=True)
    normed = (centered * lax.rsqrt(variance + 1e-05)).reshape(row_count, inner)
    return (normed * norm_gain * jax.nn.silu(output_gate.astype(jnp.float32))).astype(jnp.bfloat16)


def split_seq_mesh(mesh):
    devices = np.asarray(mesh.devices)
    seq_size, tensor_size = devices.shape
    row_size = len({int(d.coords[1]) for d in devices[:, 0]})
    return Mesh(
        devices.reshape(seq_size // row_size, row_size, tensor_size), ("sx", "sy", "tensor")
    )


def solution(mesh):
    split = split_seq_mesh(mesh)
    tokens = P(("sx", "sy", "tensor"), None)
    in_specs = (tokens, tokens, tokens, tokens, tokens, P(("sx", "sy")), tokens, P())
    return jax.shard_map(
        on_device, mesh=split, in_specs=in_specs, out_specs=tokens, check_vma=False
    )
```

```python
import math

import jax
import jax.numpy as jnp
import numpy as np
from jax import lax
from jax.sharding import Mesh
from jax.sharding import PartitionSpec as P


def split_dot(wide, narrow, dims):
    high = lax.reduce_precision(wide, exponent_bits=8, mantissa_bits=7)
    low = wide - high

    def one(part):
        return lax.dot_general(
            part.astype(jnp.bfloat16),
            narrow.astype(jnp.bfloat16),
            dims,
            preferred_element_type=jnp.float32,
        )

    return one(high) + one(low)


def split_dot_left(narrow, wide, dims):
    high = lax.reduce_precision(wide, exponent_bits=8, mantissa_bits=7)
    low = wide - high

    def one(part):
        return lax.dot_general(
            narrow.astype(jnp.bfloat16),
            part.astype(jnp.bfloat16),
            dims,
            preferred_element_type=jnp.float32,
        )

    return one(high) + one(low)


def meta_row(head_dim, column_count):
    return head_dim + head_dim // column_count


def with_meta(body, row, decay, first, last, low=None):
    lane = jnp.arange(body.shape[1])[None, :]
    rows = jnp.arange(body.shape[0])[:, None]
    values = jnp.where(lane == 0, decay, jnp.where(lane == 1, first, last))
    if low is not None:
        values = jnp.where(lane == 3, low, values)
    return jnp.where((rows == row) & (lane < (3 if low is None else 4)), values, body)


def pack_summary(key_all, value_all, gate_in, cumulative, segment_ids, key_scale):
    head_dim = key_all.shape[1]
    column_count = value_all.shape[1]
    total_log = cumulative[-1]
    first_seg = segment_ids[0]
    last_seg = segment_ids[-1]
    tail_weight = jnp.exp(total_log - cumulative + gate_in) * (segment_ids == last_seg).astype(
        jnp.float32
    )
    token_weight = key_scale * tail_weight
    weighted_values = value_all.astype(jnp.float32) * token_weight[:, None]
    state = split_dot_left(key_all, weighted_values, (((0,), (0,)), ((), ())))
    norm = split_dot_left(key_all, token_weight[:, None], (((0,), (0,)), ((), ())))[:, 0]
    decay = jnp.exp(total_log) * (last_seg == first_seg).astype(jnp.float32)
    norm_rows = head_dim // column_count
    rows = meta_row(head_dim, column_count) + 1
    padded = -(-rows // 8) * 8
    filler = jnp.zeros((padded - rows + 1, column_count), jnp.float32)
    body = jnp.concatenate([state, norm.reshape(norm_rows, column_count), filler], axis=0)
    decay_high = lax.reduce_precision(decay, exponent_bits=8, mantissa_bits=7)
    return with_meta(
        body,
        meta_row(head_dim, column_count),
        decay_high,
        (first_seg + 1).astype(jnp.float32),
        (last_seg + 1).astype(jnp.float32),
        decay - decay_high,
    )


def prefix_weights(decay, first, last, mine):
    count = decay.shape[0]
    order = jnp.arange(count)
    previous_last = jnp.concatenate([jnp.zeros((1,), jnp.float32), last[:-1]])
    carry = decay * (previous_last == first).astype(jnp.float32)
    carry = jnp.where((order < mine) & (order >= 1), carry, 1.0)
    after = jnp.cumprod(carry[::-1])[::-1]
    weight = jnp.concatenate([after[1:], jnp.ones((1,), jnp.float32)])
    weight = jnp.where(order < mine, weight, 0.0)
    combined_decay = decay[0] * after[1] if count > 1 else decay[0]
    combined_last = jnp.where(mine > 0, last[jnp.maximum(mine - 1, 0)], 0.0)
    combined_first = jnp.where(mine > 0, first[0], 0.0)
    return weight, combined_decay, combined_first, combined_last


def prefix_2d(packed, head_dim, row_axis, col_axis):
    column_count = packed.shape[1]
    row = meta_row(head_dim, column_count)
    row_size = lax.axis_size(row_axis)
    me_y = lax.axis_index(row_axis)
    me_x = lax.axis_index(col_axis)

    along_row = lax.all_gather(packed.astype(jnp.bfloat16), row_axis).astype(jnp.float32)
    meta = along_row[:, row, :4]
    decay, first, last = meta[:, 0] + meta[:, 3], meta[:, 1], meta[:, 2]
    w_row, decay_r, first_r, last_r = prefix_weights(decay, first, last, me_y)
    w_all, decay_t, first_t, last_t = prefix_weights(decay, first, last, row_size)
    row_part = jnp.einsum("s,src->rc", w_row, along_row)
    row_total = with_meta(
        jnp.einsum("s,src->rc", w_all, along_row), row, decay_t, first_t, last_t
    )

    along_col = lax.all_gather(row_total, col_axis)
    meta_c = along_col[:, row, :3]
    w_col, unused_decay, unused_first, last_p = prefix_weights(
        meta_c[:, 0], meta_c[:, 1], meta_c[:, 2], me_x
    )
    col_part = jnp.einsum("s,src->rc", w_col, along_col)

    has_row = me_y > 0
    factor = jnp.where(has_row, decay_r * (last_p == first_r).astype(jnp.float32), 1.0)
    state = factor * col_part + row_part
    in_last = jnp.where(has_row, last_r, last_p)
    return state, in_last


def prefix_from_all(packed, head_dim, row_axis, col_axis):
    column_count = packed.shape[1]
    row = meta_row(head_dim, column_count)
    axes = (col_axis, row_axis)
    gathered = lax.all_gather(packed.astype(jnp.bfloat16), axes)
    meta = gathered[:, row, :4].astype(jnp.float32)
    decay, first, last = meta[:, 0] + meta[:, 3], meta[:, 1], meta[:, 2]
    me = lax.axis_index(col_axis) * lax.axis_size(row_axis) + lax.axis_index(row_axis)
    weight, unused_decay, unused_first, in_last = prefix_weights(decay, first, last, me)
    state = jnp.einsum("s,src->rc", weight, gathered.astype(jnp.float32))
    return state, in_last


def on_device(
    queries, key_rows, values, input_gate, forget_gate, segment_ids, output_gate, norm_gain
):
    tensor_size = lax.axis_size("tensor")
    row_count, inner = queries.shape
    head_count = input_gate.shape[1]
    head_dim = inner // head_count
    group_size = tensor_size // head_count
    column_count = head_dim // group_size

    def spread_heads(array, width):
        shaped = array.reshape(row_count, head_count, 1, width)
        return jnp.broadcast_to(shaped, (row_count, head_count, group_size, width)).reshape(
            row_count, tensor_size, width
        )

    half = head_dim // 2

    def halves_send(array):
        shaped = array.reshape(row_count, head_count, 1, 2, half)
        return jnp.broadcast_to(
            shaped, (row_count, head_count, group_size // 2, 2, half)
        ).reshape(row_count, tensor_size, half)

    is_even = lax.axis_index("tensor") % 2 == 0
    pairs = [(index, index ^ 1) for index in range(tensor_size)]

    def joined(own):
        other = lax.ppermute(own, "tensor", pairs)
        return jnp.where(
            is_even, jnp.concatenate([own, other], axis=1), jnp.concatenate([other, own], axis=1)
        )

    value_send = values.reshape(row_count, tensor_size, column_count)
    gate_rows = 8
    lanes = half + column_count
    gate_pair = jnp.stack([input_gate, forget_gate], axis=0)
    gate_block = jnp.broadcast_to(
        jnp.transpose(gate_pair, (2, 0, 1))[:, None], (head_count, group_size, 2, row_count)
    ).reshape(1, tensor_size, 2 * row_count)
    gate_send = jnp.pad(gate_block, ((0, gate_rows - 1), (0, 0), (0, lanes - 2 * row_count)))
    first_send = jnp.concatenate(
        [jnp.concatenate([halves_send(key_rows), value_send], axis=2), gate_send], axis=0
    )
    first_all = lax.all_to_all(first_send, "tensor", split_axis=1, concat_axis=0, tiled=True)
    first_all = first_all.reshape(tensor_size, row_count + gate_rows, lanes)
    gate_all = jnp.transpose(
        first_all[:, row_count, : 2 * row_count].reshape(tensor_size, 2, row_count), (0, 2, 1)
    ).reshape(tensor_size * row_count, 2)
    first_all = first_all[:, :row_count].reshape(tensor_size * row_count, lanes)
    value_all = first_all[:, half:]
    key_all = joined(first_all[:, :half])
    query_half = lax.all_to_all(
        halves_send(queries), "tensor", split_axis=1, concat_axis=0, tiled=True
    ).reshape(-1, half)
    query_all = joined(query_half)
    token_count = query_all.shape[0]
    gate_f = gate_all.reshape(token_count, 2).astype(jnp.float32)
    gate_in = gate_f[:, 0]
    log_forget = jax.nn.log_sigmoid(gate_f[:, 1])
    key_scale = 1.0 / math.sqrt(head_dim)
    first_seg = segment_ids[0]
    cumulative = jnp.cumsum(log_forget)

    packed = pack_summary(key_all, value_all, gate_in, cumulative, segment_ids, key_scale)
    in_packed, in_last = prefix_from_all(packed, head_dim, "sy", "sx")
    in_row = meta_row(head_dim, column_count)
    in_state = in_packed[:head_dim]
    in_norm = in_packed[head_dim:in_row].reshape(head_dim)

    token_ids = jnp.arange(token_count, dtype=jnp.int32)
    allowed = (token_ids[:, None] >= token_ids[None, :]) & (
        segment_ids[:, None] == segment_ids[None, :]
    )
    exponent = cumulative[:, None] - cumulative[None, :] + gate_in[None, :]
    weights = jnp.where(allowed, jnp.exp(jnp.where(allowed, exponent, 0.0)), 0.0)
    scores = (
        lax.dot_general(
            query_all, key_all, (((1,), (1,)), ((), ())), preferred_element_type=jnp.float32
        )
        * key_scale
    )
    weighted = weights * scores
    numerator = split_dot(weighted, value_all, (((1,), (0,)), ((), ())))
    q_norm = jnp.sum(weighted, axis=1)
    entry_factor = jnp.exp(cumulative) * (segment_ids == first_seg).astype(jnp.float32)

    linked = (in_last == (first_seg + 1).astype(jnp.float32)).astype(jnp.float32)
    scale_rows = entry_factor * linked
    numerator = numerator + scale_rows[:, None] * split_dot_left(
        query_all, in_state, (((1,), (0,)), ((), ()))
    )
    q_norm = q_norm + scale_rows * split_dot_left(
        query_all, in_norm[:, None], (((1,), (0,)), ((), ()))
    )[:, 0]
    hidden = (numerator / jnp.maximum(jnp.abs(q_norm), 1.0)[:, None]).astype(jnp.bfloat16)
    returned = lax.all_to_all(
        hidden.reshape(tensor_size, row_count, column_count),
        "tensor",
        split_axis=0,
        concat_axis=0,
        tiled=True,
    )
    hidden_f = (
        jnp.transpose(returned, (1, 0, 2)).astype(jnp.float32).reshape(row_count, head_count, head_dim)
    )
    mean_val = jnp.mean(hidden_f, axis=2, keepdims=True)
    centered = hidden_f - mean_val
    variance = jnp.mean(centered * centered, axis=2, keepdims=True)
    normed = (centered * lax.rsqrt(variance + 1e-05)).reshape(row_count, inner)
    return (normed * norm_gain * jax.nn.silu(output_gate.astype(jnp.float32))).astype(jnp.bfloat16)


def split_seq_mesh(mesh):
    devices = np.asarray(mesh.devices)
    seq_size, tensor_size = devices.shape
    row_size = len({int(d.coords[1]) for d in devices[:, 0]})
    return Mesh(
        devices.reshape(seq_size // row_size, row_size, tensor_size), ("sx", "sy", "tensor")
    )


def solution(mesh):
    split = split_seq_mesh(mesh)
    tokens = P(("sx", "sy", "tensor"), None)
    in_specs = (tokens, tokens, tokens, tokens, tokens, P(("sx", "sy")), tokens, P())
    return jax.shard_map(
        on_device, mesh=split, in_specs=in_specs, out_specs=tokens, check_vma=False
    )
```

```python
import math

import jax
import jax.numpy as jnp
import numpy as np
from jax import lax
from jax.sharding import Mesh
from jax.sharding import PartitionSpec as P


def split_dot(wide, narrow, dims):
    high = lax.reduce_precision(wide, exponent_bits=8, mantissa_bits=7)
    low = wide - high

    def one(part):
        return lax.dot_general(
            part.astype(jnp.bfloat16),
            narrow.astype(jnp.bfloat16),
            dims,
            preferred_element_type=jnp.float32,
        )

    return one(high) + one(low)


def split_dot_left(narrow, wide, dims):
    high = lax.reduce_precision(wide, exponent_bits=8, mantissa_bits=7)
    low = wide - high

    def one(part):
        return lax.dot_general(
            narrow.astype(jnp.bfloat16),
            part.astype(jnp.bfloat16),
            dims,
            preferred_element_type=jnp.float32,
        )

    return one(high) + one(low)


def meta_row(head_dim, column_count):
    return head_dim + head_dim // column_count


def with_meta(body, row, decay, first, last, low=None):
    lane = jnp.arange(body.shape[1])[None, :]
    rows = jnp.arange(body.shape[0])[:, None]
    values = jnp.where(lane == 0, decay, jnp.where(lane == 1, first, last))
    if low is not None:
        values = jnp.where(lane == 3, low, values)
    return jnp.where((rows == row) & (lane < (3 if low is None else 4)), values, body)


def pack_summary(key_all, value_all, gate_in, cumulative, segment_ids, key_scale):
    head_dim = key_all.shape[1]
    column_count = value_all.shape[1]
    total_log = cumulative[-1]
    first_seg = segment_ids[0]
    last_seg = segment_ids[-1]
    tail_weight = jnp.exp(total_log - cumulative + gate_in) * (segment_ids == last_seg).astype(
        jnp.float32
    )
    token_weight = key_scale * tail_weight
    weighted_values = value_all.astype(jnp.float32) * token_weight[:, None]
    state = split_dot_left(key_all, weighted_values, (((0,), (0,)), ((), ())))
    norm = jnp.sum(key_all.astype(jnp.float32) * token_weight[:, None], axis=0)
    decay = jnp.exp(total_log) * (last_seg == first_seg).astype(jnp.float32)
    norm_rows = head_dim // column_count
    rows = meta_row(head_dim, column_count) + 1
    padded = -(-rows // 8) * 8
    filler = jnp.zeros((padded - rows + 1, column_count), jnp.float32)
    body = jnp.concatenate([state, norm.reshape(norm_rows, column_count), filler], axis=0)
    decay_high = lax.reduce_precision(decay, exponent_bits=8, mantissa_bits=7)
    return with_meta(
        body,
        meta_row(head_dim, column_count),
        decay_high,
        (first_seg + 1).astype(jnp.float32),
        (last_seg + 1).astype(jnp.float32),
        decay - decay_high,
    )


def prefix_weights(decay, first, last, mine):
    count = decay.shape[0]
    order = jnp.arange(count)
    previous_last = jnp.concatenate([jnp.zeros((1,), jnp.float32), last[:-1]])
    carry = decay * (previous_last == first).astype(jnp.float32)
    carry = jnp.where((order < mine) & (order >= 1), carry, 1.0)
    after = jnp.cumprod(carry[::-1])[::-1]
    weight = jnp.concatenate([after[1:], jnp.ones((1,), jnp.float32)])
    weight = jnp.where(order < mine, weight, 0.0)
    combined_decay = decay[0] * after[1] if count > 1 else decay[0]
    combined_last = jnp.where(mine > 0, last[jnp.maximum(mine - 1, 0)], 0.0)
    combined_first = jnp.where(mine > 0, first[0], 0.0)
    return weight, combined_decay, combined_first, combined_last


def prefix_2d(packed, head_dim, row_axis, col_axis):
    column_count = packed.shape[1]
    row = meta_row(head_dim, column_count)
    row_size = lax.axis_size(row_axis)
    me_y = lax.axis_index(row_axis)
    me_x = lax.axis_index(col_axis)

    along_row = lax.all_gather(packed.astype(jnp.bfloat16), row_axis).astype(jnp.float32)
    meta = along_row[:, row, :4]
    decay, first, last = meta[:, 0] + meta[:, 3], meta[:, 1], meta[:, 2]
    w_row, decay_r, first_r, last_r = prefix_weights(decay, first, last, me_y)
    w_all, decay_t, first_t, last_t = prefix_weights(decay, first, last, row_size)
    row_part = jnp.einsum("s,src->rc", w_row, along_row)
    row_total = with_meta(
        jnp.einsum("s,src->rc", w_all, along_row), row, decay_t, first_t, last_t
    )

    along_col = lax.all_gather(row_total, col_axis)
    meta_c = along_col[:, row, :3]
    w_col, unused_decay, unused_first, last_p = prefix_weights(
        meta_c[:, 0], meta_c[:, 1], meta_c[:, 2], me_x
    )
    col_part = jnp.einsum("s,src->rc", w_col, along_col)

    has_row = me_y > 0
    factor = jnp.where(has_row, decay_r * (last_p == first_r).astype(jnp.float32), 1.0)
    state = factor * col_part + row_part
    in_last = jnp.where(has_row, last_r, last_p)
    return state, in_last


def prefix_from_all(packed, head_dim, row_axis, col_axis):
    column_count = packed.shape[1]
    row = meta_row(head_dim, column_count)
    axes = (col_axis, row_axis)
    gathered = lax.all_gather(packed.astype(jnp.bfloat16), axes)
    meta = gathered[:, row, :4].astype(jnp.float32)
    decay, first, last = meta[:, 0] + meta[:, 3], meta[:, 1], meta[:, 2]
    me = lax.axis_index(col_axis) * lax.axis_size(row_axis) + lax.axis_index(row_axis)
    weight, unused_decay, unused_first, in_last = prefix_weights(decay, first, last, me)
    state = jnp.einsum("s,src->rc", weight, gathered.astype(jnp.float32))
    return state, in_last


def on_device(
    queries, key_rows, values, input_gate, forget_gate, segment_ids, output_gate, norm_gain
):
    tensor_size = lax.axis_size("tensor")
    row_count, inner = queries.shape
    head_count = input_gate.shape[1]
    head_dim = inner // head_count
    group_size = tensor_size // head_count
    column_count = head_dim // group_size

    def spread_heads(array, width):
        shaped = array.reshape(row_count, head_count, 1, width)
        return jnp.broadcast_to(shaped, (row_count, head_count, group_size, width)).reshape(
            row_count, tensor_size, width
        )

    half = head_dim // 2

    def halves_send(array):
        shaped = array.reshape(row_count, head_count, 1, 2, half)
        return jnp.broadcast_to(
            shaped, (row_count, head_count, group_size // 2, 2, half)
        ).reshape(row_count, tensor_size, half)

    is_even = lax.axis_index("tensor") % 2 == 0
    pairs = [(index, index ^ 1) for index in range(tensor_size)]

    def joined(own):
        other = lax.ppermute(own, "tensor", pairs)
        return jnp.where(
            is_even, jnp.concatenate([own, other], axis=1), jnp.concatenate([other, own], axis=1)
        )

    value_send = values.reshape(row_count, tensor_size, column_count)
    gate_rows = 8
    lanes = half + column_count
    gate_pair = jnp.stack([input_gate, forget_gate], axis=0)
    gate_block = jnp.broadcast_to(
        jnp.transpose(gate_pair, (2, 0, 1))[:, None], (head_count, group_size, 2, row_count)
    ).reshape(1, tensor_size, 2 * row_count)
    gate_send = jnp.pad(gate_block, ((0, gate_rows - 1), (0, 0), (0, lanes - 2 * row_count)))
    first_send = jnp.concatenate(
        [jnp.concatenate([halves_send(key_rows), value_send], axis=2), gate_send], axis=0
    )
    first_all = lax.all_to_all(first_send, "tensor", split_axis=1, concat_axis=0, tiled=True)
    first_all = first_all.reshape(tensor_size, row_count + gate_rows, lanes)
    gate_all = jnp.transpose(
        first_all[:, row_count, : 2 * row_count].reshape(tensor_size, 2, row_count), (0, 2, 1)
    ).reshape(tensor_size * row_count, 2)
    first_all = first_all[:, :row_count].reshape(tensor_size * row_count, lanes)
    value_all = first_all[:, half:]
    key_all = joined(first_all[:, :half])
    query_half = lax.all_to_all(
        halves_send(queries), "tensor", split_axis=1, concat_axis=0, tiled=True
    ).reshape(-1, half)
    query_all = joined(query_half)
    token_count = query_all.shape[0]
    gate_f = gate_all.reshape(token_count, 2).astype(jnp.float32)
    gate_in = gate_f[:, 0]
    log_forget = jax.nn.log_sigmoid(gate_f[:, 1])
    key_scale = 1.0 / math.sqrt(head_dim)
    first_seg = segment_ids[0]
    cumulative = jnp.cumsum(log_forget)

    packed = pack_summary(key_all, value_all, gate_in, cumulative, segment_ids, key_scale)
    in_packed, in_last = prefix_from_all(packed, head_dim, "sy", "sx")
    in_row = meta_row(head_dim, column_count)
    in_state = in_packed[:head_dim]
    in_norm = in_packed[head_dim:in_row].reshape(head_dim)

    token_ids = jnp.arange(token_count, dtype=jnp.int32)
    allowed = (token_ids[:, None] >= token_ids[None, :]) & (
        segment_ids[:, None] == segment_ids[None, :]
    )
    exponent = cumulative[:, None] - cumulative[None, :] + gate_in[None, :]
    weights = jnp.where(allowed, jnp.exp(jnp.where(allowed, exponent, 0.0)), 0.0)
    scores = (
        lax.dot_general(
            query_all, key_all, (((1,), (1,)), ((), ())), preferred_element_type=jnp.float32
        )
        * key_scale
    )
    weighted = weights * scores
    numerator = split_dot(weighted, value_all, (((1,), (0,)), ((), ())))
    q_norm = jnp.sum(weighted, axis=1)
    entry_factor = jnp.exp(cumulative) * (segment_ids == first_seg).astype(jnp.float32)

    linked = (in_last == (first_seg + 1).astype(jnp.float32)).astype(jnp.float32)
    scale_rows = entry_factor * linked
    numerator = numerator + scale_rows[:, None] * split_dot_left(
        query_all, in_state, (((1,), (0,)), ((), ()))
    )
    q_norm = q_norm + scale_rows * split_dot_left(
        query_all, in_norm[:, None], (((1,), (0,)), ((), ()))
    )[:, 0]
    hidden = (numerator / jnp.maximum(jnp.abs(q_norm), 1.0)[:, None]).astype(jnp.bfloat16)
    returned = lax.all_to_all(
        hidden.reshape(tensor_size, row_count, column_count),
        "tensor",
        split_axis=0,
        concat_axis=0,
        tiled=True,
    )
    hidden_f = (
        jnp.transpose(returned, (1, 0, 2)).astype(jnp.float32).reshape(row_count, head_count, head_dim)
    )
    mean_val = jnp.mean(hidden_f, axis=2, keepdims=True)
    centered = hidden_f - mean_val
    variance = jnp.mean(centered * centered, axis=2, keepdims=True)
    normed = (centered * lax.rsqrt(variance + 1e-05)).reshape(row_count, inner)
    return (normed * norm_gain * jax.nn.silu(output_gate.astype(jnp.float32))).astype(jnp.bfloat16)


def split_seq_mesh(mesh):
    devices = np.asarray(mesh.devices)
    seq_size, tensor_size = devices.shape
    row_size = len({int(d.coords[1]) for d in devices[:, 0]})
    return Mesh(
        devices.reshape(seq_size // row_size, row_size, tensor_size), ("sx", "sy", "tensor")
    )


def solution(mesh):
    split = split_seq_mesh(mesh)
    tokens = P(("sx", "sy", "tensor"), None)
    in_specs = (tokens, tokens, tokens, tokens, tokens, P(("sx", "sy")), tokens, P())
    return jax.shard_map(
        on_device, mesh=split, in_specs=in_specs, out_specs=tokens, check_vma=False
    )
```
